1024 devices in a mesh: ctx: 128 (over z, y), ch: 8 (over x, core).
Axes of the slice: x: 4, y: 4, z: 32, core: 2. Of those that a mesh axis runs over, the one named last changes fastest.
Arguments:
- features: bfloat16 [3, 16384, 8192], P(None, 'ctx', 'ch'), may hold values from -6 to 6
- grad_rows: bfloat16 [16384, 8192], P(('ctx', 'ch')), may hold values from -6 to 6
- conv_taps: float32 [3, 3, 8192], P(None, None, 'ch'), may hold values from -3.5 to 3.5
- decay_rate: float32 [16, 8192], P(None, 'ch'), may hold values from 0 to 1, as said below
- residue: float32 [16, 8192], P(None, 'ch'), may hold values from -1.5 to 1.5
- skip_gain: float32 [8192], P('ch'), may hold values from -1 to 1
Outputs:
- grad_features: bfloat16 [3, 16384, 8192], P(None, 'ctx', 'ch')
The draws below stay inside these ranges and needn't reach their ends.
Inputs may be any that keep to these rules, and one draw needn't show every extreme that they name: `decay_rate`: positive decay rates.
All inputs are finite; a program needn't handle non-finite values.
Results may differ from the reference program's by a relative error of at most 0.00125.
Values may be sent and summed in bfloat16 or wider, within the bound.
No kernel may reach another device: no remote copies, remote signals or barrier semaphores. Data moves between devices by JAX's collectives and lax.ppermute only.
A program may use at most 128 MiB of HBM per device.

```python
import math
import jax
import jax.numpy as jnp
from jax import lax

D = 8192
MODES = 16
TAPS = 3
TOKENS = 16384


def draw_decay_rate(key, part):
    key_pick, key_slow, key_fast = jax.random.split(key, 3)
    slow_share = 0.5
    picker = jax.random.uniform(key_pick, (MODES, D), jnp.float32)
    slow_rates = jnp.exp(jax.random.uniform(key_slow, (MODES, D), jnp.float32, math.log(0.2), math.log(16.0))) / TOKENS
    fast_rates = jnp.exp(jax.random.uniform(key_fast, (MODES, D), jnp.float32, math.log(0.001), math.log(0.1)))
    return jnp.where(picker < slow_share, slow_rates, fast_rates).astype(jnp.float32)


def block_scale(rng, extent, cuts, least, top_value):
    loudness = 1.0
    for dim, blocks in cuts:
        steps = jax.random.uniform(jax.random.fold_in(jax.random.fold_in(rng, 6), dim), (blocks,), jnp.float32, least / len(cuts), top_value / len(cuts))
        loudness = loudness * jnp.repeat(jnp.exp(steps), extent[dim] // blocks).reshape((-1,) + (1,) * (len(extent) - 1 - dim))
    return loudness


def noise(stream_key, shape, deviation, reach, cuts=(), held_as=jnp.bfloat16):
    array = deviation * jax.random.normal(stream_key, shape, jnp.float32)
    if cuts:
        array = array * block_scale(stream_key, shape, cuts, -0.22, 0.18)
    return jnp.clip(array, -reach, reach).astype(held_as)


def setup_inputs(seed: int = 0) -> dict:
    keys = jax.random.split(jax.random.key(seed), 7)
    features = noise(keys[0], (3, TOKENS, D), 1.0, 6.0, ((1, 128), (2, 8)))
    grad_rows = noise(keys[1], (TOKENS, D), 1.0, 6.0, ((0, 1024),))
    conv_taps = noise(keys[2], (3, TAPS, D), TAPS ** -0.5, 3.5, ((2, 8),), jnp.float32)
    decay_rate = draw_decay_rate(jax.random.fold_in(keys[6], 71), 0)
    residue = noise(keys[4], (MODES, D), MODES ** -0.5, 1.5, ((1, 8),), jnp.float32)
    skip_gain = jnp.clip(jax.random.uniform(keys[5], (D,), jnp.float32, -1.0, 1.0) * block_scale(keys[5], (D,), ((0, 8),), -0.4, 0.0), -1.0, 1.0)
    return {"features": features, "grad_rows": grad_rows, "conv_taps": conv_taps, "decay_rate": decay_rate, "residue": residue, "skip_gain": skip_gain}


def local_pass(signal, decay_rate, gain_in, gain_out):
    total_len, width_dev = signal.shape
    block_len = math.gcd(16, total_len)
    block_count = total_len // block_len
    offsets = jnp.arange(block_len, dtype=jnp.float32)
    rates = decay_rate[None]
    decay_in = jnp.exp(-rates * (block_len - 1.0 - offsets)[:, None, None]) * gain_in[None]
    decay_out = jnp.exp(-rates * (offsets + 1.0)[:, None, None]) * gain_out[None]
    kernel = lax.optimization_barrier(jnp.sum(jnp.exp(-rates * offsets[:, None, None]) * (gain_in * gain_out)[None], axis=1))
    lag_index = jnp.arange(block_len, dtype=jnp.int32)[:, None] - jnp.arange(block_len, dtype=jnp.int32)[None, :]
    toeplitz = jnp.where(lag_index[:, :, None] >= 0, kernel[jnp.maximum(lag_index, 0)], jnp.zeros_like(kernel[:1, None]))
    blocks = signal.reshape(block_count, block_len, width_dev)
    local_out = lax.optimization_barrier(jnp.sum(blocks[:, None, :, :] * toeplitz[None], axis=2))
    block_ends = lax.optimization_barrier(jnp.sum(blocks[:, :, None, :] * decay_in[None], axis=1))
    block_decay = jnp.exp(-decay_rate * block_len)

    def advance(state_now, entry):
        return (block_decay * state_now + entry, state_now)
    final_state, block_starts = lax.scan(advance, jnp.zeros_like(decay_rate), block_ends)
    return (local_out, block_starts, final_state, decay_out)

def finish(pieces, decay_rate, initial):
    local_out, block_starts, final_state, decay_out = pieces
    block_count, block_len, width_dev = local_out.shape
    anchors = jnp.arange(block_count, dtype=jnp.float32) * block_len
    powers = jnp.exp(-decay_rate[None] * anchors[:, None, None])
    states = block_starts + powers * initial[None]
    result = local_out + lax.optimization_barrier(jnp.sum(decay_out[None] * states[:, None], axis=2))
    return result.reshape(block_count * block_len, width_dev)

def causal_taps(signal, tap_weights):
    rim_rows = tap_weights.shape[0] - 1
    total_len = signal.shape[0]
    padded = jnp.pad(signal, ((rim_rows, 0), (0, 0)))
    result = tap_weights[0][None] * padded[rim_rows:rim_rows + total_len]
    for shift_by in range(1, rim_rows + 1):
        result = result + tap_weights[shift_by][None] * padded[rim_rows - shift_by:rim_rows - shift_by + total_len]
    return result

def anticausal_taps(signal, tap_weights):
    rim_rows = tap_weights.shape[0] - 1
    total_len = signal.shape[0]
    padded = jnp.pad(signal, ((0, rim_rows), (0, 0)))
    result = tap_weights[0][None] * padded[0:total_len]
    for shift_by in range(1, rim_rows + 1):
        result = result + tap_weights[shift_by][None] * padded[shift_by:shift_by + total_len]
    return result

def one_group(feats, grad_out, tap_weights, decay_rate, residue, skip_gain):
    signals = feats.astype(jnp.float32)
    queries = causal_taps(signals[0], tap_weights[0])
    keys_feat = causal_taps(signals[1], tap_weights[1])
    values_feat = causal_taps(signals[2], tap_weights[2])
    gain_in = jnp.sqrt(-jnp.expm1(-2.0 * decay_rate))
    product = keys_feat * values_feat
    zero_state = jnp.zeros_like(decay_rate)
    forward = local_pass(product, decay_rate, gain_in, residue)
    conv_out = finish(forward, decay_rate, zero_state) + skip_gain[None] * product
    grad_float = grad_out.astype(jnp.float32)
    grad_query = grad_float * conv_out
    grad_conv = grad_float * queries
    backward = local_pass(grad_conv[::-1], decay_rate, jnp.ones_like(decay_rate), residue * gain_in)
    grad_product = finish(backward, decay_rate, zero_state)[::-1] + skip_gain[None] * grad_conv
    grad_key = grad_product * values_feat
    grad_value = grad_product * keys_feat
    result = jnp.stack([anticausal_taps(grad_query, tap_weights[0]), anticausal_taps(grad_key, tap_weights[1]), anticausal_taps(grad_value, tap_weights[2])])
    return result.astype(jnp.bfloat16)

def reference(features, grad_rows, conv_taps, decay_rate, residue, skip_gain):
    total_len = features.shape[1]
    width_all = features.shape[2]
    tap_count = conv_taps.shape[1]
    mode_count = decay_rate.shape[0]
    group_width = math.gcd(1024, width_all)
    group_count = width_all // group_width
    feats = features.reshape(3, total_len, group_count, group_width).transpose(2, 0, 1, 3)
    grads = grad_rows.reshape(total_len, group_count, group_width).transpose(1, 0, 2)
    tap_groups = conv_taps.reshape(3, tap_count, group_count, group_width).transpose(2, 0, 1, 3)
    rate_groups = decay_rate.reshape(mode_count, group_count, group_width).transpose(1, 0, 2)
    residue_groups = residue.reshape(mode_count, group_count, group_width).transpose(1, 0, 2)
    skip_groups = skip_gain.reshape(group_count, group_width)
    result = lax.map(lambda pieces: one_group(*pieces), (feats, grads, tap_groups, rate_groups, residue_groups, skip_groups))
    return result.transpose(1, 2, 0, 3).reshape(3, total_len, width_all)
```

```python
import math

import jax
import jax.numpy as jnp
from jax import lax
from jax.sharding import PartitionSpec as P


def shifted(block, axis, distance):
    devices = range(lax.axis_size(axis))
    route = [(i - distance, i) for i in devices if i - distance in devices]
    return lax.ppermute(block, axis, route)


def carried_in(final, decay_rate, length, backward):
    count = lax.axis_size("ctx")
    step = -1 if backward else 1
    factor = jnp.exp(-decay_rate * length)
    total = shifted(final, "ctx", step)
    if count > 2:
        total = total + factor * shifted(final, "ctx", 2 * step)
    distance = 2
    while distance < count:
        power = jnp.exp(-decay_rate * (length * distance))
        total = total + power * shifted(total, "ctx", distance * step)
        distance *= 2
    return total


def local_pass(signal, decay_rate, gain_in, gain_out):
    total_len, width_dev = signal.shape
    block_len = math.gcd(16, total_len)
    block_count = total_len // block_len
    offsets = jnp.arange(block_len, dtype=jnp.float32)
    rates = decay_rate[None]
    decay_in = jnp.exp(-rates * (block_len - 1.0 - offsets)[:, None, None]) * gain_in[None]
    decay_out = jnp.exp(-rates * (offsets + 1.0)[:, None, None]) * gain_out[None]
    kernel = jnp.sum(jnp.exp(-rates * offsets[:, None, None]) * (gain_in * gain_out)[None], axis=1)
    lag_index = (
        jnp.arange(block_len, dtype=jnp.int32)[:, None]
        - jnp.arange(block_len, dtype=jnp.int32)[None, :]
    )
    toeplitz = jnp.where(
        lag_index[:, :, None] >= 0,
        kernel[jnp.maximum(lag_index, 0)],
        jnp.zeros_like(kernel[:1, None]),
    )
    blocks = signal.reshape(block_count, block_len, width_dev)
    local_out = jnp.sum(blocks[:, None, :, :] * toeplitz[None], axis=2)
    block_ends = jnp.sum(blocks[:, :, None, :] * decay_in[None], axis=1)
    block_decay = jnp.exp(-decay_rate * block_len)

    def advance(state_now, entry):
        return (block_decay * state_now + entry, state_now)

    final_state, block_starts = lax.scan(advance, jnp.zeros_like(decay_rate), block_ends)
    return (local_out, block_starts, final_state, decay_out)


def finish(pieces, decay_rate, initial):
    local_out, block_starts, final_state, decay_out = pieces
    block_count, block_len, width_dev = local_out.shape
    anchors = jnp.arange(block_count, dtype=jnp.float32) * block_len
    powers = jnp.exp(-decay_rate[None] * anchors[:, None, None])
    states = block_starts + powers * initial[None]
    result = local_out + jnp.sum(decay_out[None] * states[:, None], axis=2)
    return result.reshape(block_count * block_len, width_dev)


def per_device(features, grad_rows, conv_taps, decay_rate, residue, skip_gain):
    length = features.shape[1]
    rim_rows = conv_taps.shape[1] - 1
    grad_out = lax.all_to_all(grad_rows, "ch", split_axis=1, concat_axis=0, tiled=True)
    last_rows = features[:, length - rim_rows :, :]
    before = shifted(last_rows, "ctx", 1)
    extended = jnp.concatenate([before, features], axis=1)
    featurized = conv_taps[:, 0, None, :] * extended[:, rim_rows : rim_rows + length, :]
    for shift_by in range(1, rim_rows + 1):
        featurized = (
            featurized
            + conv_taps[:, shift_by, None, :]
            * extended[:, rim_rows - shift_by : rim_rows - shift_by + length, :]
        )
    queries = featurized[0]
    keys_feat = featurized[1]
    values_feat = featurized[2]
    gain_in = jnp.sqrt(-jnp.expm1(-2.0 * decay_rate))
    product = keys_feat * values_feat
    forward = local_pass(product, decay_rate, gain_in, residue)
    grad_float = grad_out.astype(jnp.float32)
    grad_conv = grad_float * queries
    backward = local_pass(grad_conv[::-1], decay_rate, jnp.ones_like(decay_rate), residue * gain_in)

    state_in = carried_in(forward[2], decay_rate, length, False)
    adjoint_in = carried_in(backward[2], decay_rate, length, True)
    conv_out = finish(forward, decay_rate, state_in) + skip_gain[None] * product
    grad_query = grad_float * conv_out
    grad_product = finish(backward, decay_rate, adjoint_in)[::-1] + skip_gain[None] * grad_conv
    grad_key = grad_product * values_feat
    grad_value = grad_product * keys_feat
    grad_stack = jnp.stack([grad_query, grad_key, grad_value])
    following = shifted(grad_stack[:, :rim_rows, :], "ctx", -1)
    padded = jnp.concatenate([grad_stack, following], axis=1)
    result = conv_taps[:, 0, None, :] * padded[:, 0:length, :]
    for shift_by in range(1, rim_rows + 1):
        result = (
            result + conv_taps[:, shift_by, None, :] * padded[:, shift_by : shift_by + length, :]
        )
    return result.astype(jnp.bfloat16)


def solution(mesh):
    in_specs = (
        P(None, "ctx", "ch"),
        P(("ctx", "ch"), None),
        P(None, None, "ch"),
        P(None, "ch"),
        P(None, "ch"),
        P("ch"),
    )
    out_specs = P(None, "ctx", "ch")
    return jax.shard_map(
        per_device, mesh=mesh, in_specs=in_specs, out_specs=out_specs, check_vma=False
    )
```

```python
import math

import jax
import jax.numpy as jnp
from jax import lax
from jax.sharding import PartitionSpec as P


def shifted(block, axis, distance):
    devices = range(lax.axis_size(axis))
    route = [(i - distance, i) for i in devices if i - distance in devices]
    return lax.ppermute(block, axis, route)


def carried_in(finals, decay_rate, length, radix=4):
    count = lax.axis_size("ctx")
    directions = (1, -1)

    def decay(distance):
        return jnp.exp(-decay_rate * (length * distance))

    totals = []
    for final, step in zip(finals, directions):
        total = shifted(final, "ctx", step)
        for lag in range(2, min(radix, count - 1) + 1):
            total = total + decay(lag - 1) * shifted(final, "ctx", lag * step)
        totals.append(total)
    window = radix
    while window < count:
        totals = list(lax.optimization_barrier(tuple(totals)))
        grown = []
        for total, step in zip(totals, directions):
            extra = total
            for part in range(1, radix):
                if part * window >= count:
                    break
                distance = part * window
                extra = extra + decay(distance) * shifted(total, "ctx", distance * step)
            grown.append(extra)
        totals = grown
        window *= radix
    return totals


def local_pass(signal, decay_rate, gain_in, gain_out):
    total_len, width_dev = signal.shape
    block_len = math.gcd(16, total_len)
    block_count = total_len // block_len
    offsets = jnp.arange(block_len, dtype=jnp.float32)
    rates = decay_rate[None]
    decay_in = jnp.exp(-rates * (block_len - 1.0 - offsets)[:, None, None]) * gain_in[None]
    decay_out = jnp.exp(-rates * (offsets + 1.0)[:, None, None]) * gain_out[None]
    kernel = jnp.sum(jnp.exp(-rates * offsets[:, None, None]) * (gain_in * gain_out)[None], axis=1)
    lag_index = (
        jnp.arange(block_len, dtype=jnp.int32)[:, None]
        - jnp.arange(block_len, dtype=jnp.int32)[None, :]
    )
    toeplitz = jnp.where(
        lag_index[:, :, None] >= 0,
        kernel[jnp.maximum(lag_index, 0)],
        jnp.zeros_like(kernel[:1, None]),
    )
    blocks = signal.reshape(block_count, block_len, width_dev)
    local_out = jnp.sum(blocks[:, None, :, :] * toeplitz[None], axis=2)
    block_ends = jnp.sum(blocks[:, :, None, :] * decay_in[None], axis=1)
    block_decay = jnp.exp(-decay_rate * block_len)

    def advance(state_now, entry):
        return (block_decay * state_now + entry, state_now)

    final_state, block_starts = lax.scan(advance, jnp.zeros_like(decay_rate), block_ends)
    return (local_out, block_starts, final_state, decay_out)


def finish(pieces, decay_rate, initial):
    local_out, block_starts, final_state, decay_out = pieces
    block_count, block_len, width_dev = local_out.shape
    anchors = jnp.arange(block_count, dtype=jnp.float32) * block_len
    powers = jnp.exp(-decay_rate[None] * anchors[:, None, None])
    states = block_starts + powers * initial[None]
    result = local_out + jnp.sum(decay_out[None] * states[:, None], axis=2)
    return result.reshape(block_count * block_len, width_dev)


def per_device(features, grad_rows, conv_taps, decay_rate, residue, skip_gain):
    length = features.shape[1]
    rim_rows = conv_taps.shape[1] - 1
    grad_out = lax.all_to_all(grad_rows, "ch", split_axis=1, concat_axis=0, tiled=True)
    last_rows = features[:, length - rim_rows :, :]
    before = shifted(last_rows, "ctx", 1)
    extended = jnp.concatenate([before, features], axis=1)
    featurized = conv_taps[:, 0, None, :] * extended[:, rim_rows : rim_rows + length, :]
    for shift_by in range(1, rim_rows + 1):
        featurized = (
            featurized
            + conv_taps[:, shift_by, None, :]
            * extended[:, rim_rows - shift_by : rim_rows - shift_by + length, :]
        )
    queries = featurized[0]
    keys_feat = featurized[1]
    values_feat = featurized[2]
    gain_in = jnp.sqrt(-jnp.expm1(-2.0 * decay_rate))
    product = keys_feat * values_feat
    forward = local_pass(product, decay_rate, gain_in, residue)
    grad_float = grad_out.astype(jnp.float32)
    grad_conv = grad_float * queries
    backward = local_pass(grad_conv[::-1], decay_rate, jnp.ones_like(decay_rate), residue * gain_in)

    state_in, adjoint_in = carried_in((forward[2], backward[2]), decay_rate, length)
    conv_out = finish(forward, decay_rate, state_in) + skip_gain[None] * product
    grad_query = grad_float * conv_out
    grad_product = finish(backward, decay_rate, adjoint_in)[::-1] + skip_gain[None] * grad_conv
    grad_key = grad_product * values_feat
    grad_value = grad_product * keys_feat
    grad_stack = jnp.stack([grad_query, grad_key, grad_value])
    following = shifted(grad_stack[:, :rim_rows, :], "ctx", -1)
    padded = jnp.concatenate([grad_stack, following], axis=1)
    result = conv_taps[:, 0, None, :] * padded[:, 0:length, :]
    for shift_by in range(1, rim_rows + 1):
        result = (
            result + conv_taps[:, shift_by, None, :] * padded[:, shift_by : shift_by + length, :]
        )
    return result.astype(jnp.bfloat16)


def solution(mesh):
    in_specs = (
        P(None, "ctx", "ch"),
        P(("ctx", "ch"), None),
        P(None, None, "ch"),
        P(None, "ch"),
        P(None, "ch"),
        P("ch"),
    )
    out_specs = P(None, "ctx", "ch")
    return jax.shard_map(
        per_device, mesh=mesh, in_specs=in_specs, out_specs=out_specs, check_vma=False
    )
```

```python
import math

import jax
import jax.numpy as jnp
from jax import lax
from jax.sharding import PartitionSpec as P


def shifted(block, axis, distance):
    devices = range(lax.axis_size(axis))
    route = [(i - distance, i) for i in devices if i - distance in devices]
    return lax.ppermute(block, axis, route)


def routed(block, pairs):
    return lax.ppermute(block, "ctx", pairs)


def within_group(count, group, offset):
    return [(i, (i // group) * group + (i % group + offset) % group) for i in range(count)]


def along_groups(count, distance):
    return [(i, i + distance) for i in range(count) if 0 <= i + distance < count]


def pick(stack, index):
    choice = jnp.arange(stack.shape[0])[None, :] == index[:, None]
    return jnp.sum(jnp.where(choice[:, :, None, None], stack[None], 0.0), axis=1)


def carried_in(finals, decay_rate, length):
    count = lax.axis_size("ctx")
    group = 4 if count % 4 == 0 and count > 4 else 1
    modes, width = decay_rate.shape
    part = modes // group
    mine = lax.axis_index("ctx") % group
    rates = lax.dynamic_index_in_dim(decay_rate.reshape(group, part, width), mine, 0, False)

    def decay(distance):
        return jnp.exp(-rates * (length * distance))

    directions = (1, -1)
    sent = [final.reshape(group, part, width) for final in finals]
    received = []
    for pieces in sent:
        got = [lax.dynamic_index_in_dim(pieces, mine, 0, False)]
        for offset in range(1, group):
            chunk = lax.dynamic_index_in_dim(pieces, (mine + offset) % group, 0, False)
            got.append(routed(chunk, within_group(count, group, offset)))
        received.append(jnp.stack(got))
    members = jnp.arange(group)
    index = (mine - members) % group
    locals_, totals = [], []
    for stack, step in zip(received, directions):
        member = pick(stack, index)
        if step < 0:
            member = member[::-1]
        prefix = [jnp.zeros_like(member[0])]
        for position in range(1, group):
            prefix.append(decay(1.0) * prefix[-1] + member[position - 1])
        total = decay(1.0) * prefix[-1] + member[group - 1]
        if step < 0:
            prefix = prefix[::-1]
        locals_.append(prefix)
        totals.append(total)
    groups = count // group
    totals = list(lax.optimization_barrier(tuple(totals)))
    entering = []
    for total, step in zip(totals, directions):
        value = routed(total, along_groups(count, group * step))
        if groups > 2:
            value = value + decay(group) * routed(total, along_groups(count, 2 * group * step))
        entering.append(value)
    distance = 2
    while distance < groups:
        entering = list(lax.optimization_barrier(tuple(entering)))
        entering = [
            value + decay(group * distance) * routed(value, along_groups(count, group * distance * step))
            for value, step in zip(entering, directions)
        ]
        distance *= 2
    results = []
    for prefix, value, step in zip(locals_, entering, directions):
        outs = []
        for position in range(group):
            lag = position if step > 0 else group - 1 - position
            outs.append(prefix[position] + decay(lag) * value)
        results.append(jnp.stack(outs))
    results = list(lax.optimization_barrier(tuple(results)))
    finals_out = []
    for stack in results:
        got = [lax.dynamic_index_in_dim(stack, mine, 0, False)]
        for offset in range(1, group):
            chunk = lax.dynamic_index_in_dim(stack, (mine + offset) % group, 0, False)
            got.append(routed(chunk, within_group(count, group, offset)))
        quarter = pick(jnp.stack(got), index)
        finals_out.append(quarter.reshape(modes, width))
    return finals_out


def local_pass(signal, decay_rate, gain_in, gain_out):
    total_len, width_dev = signal.shape
    block_len = math.gcd(16, total_len)
    block_count = total_len // block_len
    offsets = jnp.arange(block_len, dtype=jnp.float32)
    rates = decay_rate[None]
    decay_in = jnp.exp(-rates * (block_len - 1.0 - offsets)[:, None, None]) * gain_in[None]
    decay_out = jnp.exp(-rates * (offsets + 1.0)[:, None, None]) * gain_out[None]
    kernel = jnp.sum(jnp.exp(-rates * offsets[:, None, None]) * (gain_in * gain_out)[None], axis=1)
    lag_index = (
        jnp.arange(block_len, dtype=jnp.int32)[:, None]
        - jnp.arange(block_len, dtype=jnp.int32)[None, :]
    )
    toeplitz = jnp.where(
        lag_index[:, :, None] >= 0,
        kernel[jnp.maximum(lag_index, 0)],
        jnp.zeros_like(kernel[:1, None]),
    )
    blocks = signal.reshape(block_count, block_len, width_dev)
    local_out = jnp.sum(blocks[:, None, :, :] * toeplitz[None], axis=2)
    block_ends = jnp.sum(blocks[:, :, None, :] * decay_in[None], axis=1)
    block_decay = jnp.exp(-decay_rate * block_len)

    def advance(state_now, entry):
        return (block_decay * state_now + entry, state_now)

    final_state, block_starts = lax.scan(advance, jnp.zeros_like(decay_rate), block_ends)
    return (local_out, block_starts, final_state, decay_out)


def finish(pieces, decay_rate, initial):
    local_out, block_starts, final_state, decay_out = pieces
    block_count, block_len, width_dev = local_out.shape
    anchors = jnp.arange(block_count, dtype=jnp.float32) * block_len
    powers = jnp.exp(-decay_rate[None] * anchors[:, None, None])
    states = block_starts + powers * initial[None]
    result = local_out + jnp.sum(decay_out[None] * states[:, None], axis=2)
    return result.reshape(block_count * block_len, width_dev)


def per_device(features, grad_rows, conv_taps, decay_rate, residue, skip_gain):
    length = features.shape[1]
    rim_rows = conv_taps.shape[1] - 1
    grad_out = lax.all_to_all(grad_rows, "ch", split_axis=1, concat_axis=0, tiled=True)
    last_rows = features[:, length - rim_rows :, :]
    before = shifted(last_rows, "ctx", 1)
    extended = jnp.concatenate([before, features], axis=1)
    featurized = conv_taps[:, 0, None, :] * extended[:, rim_rows : rim_rows + length, :]
    for shift_by in range(1, rim_rows + 1):
        featurized = (
            featurized
            + conv_taps[:, shift_by, None, :]
            * extended[:, rim_rows - shift_by : rim_rows - shift_by + length, :]
        )
    queries = featurized[0]
    keys_feat = featurized[1]
    values_feat = featurized[2]
    gain_in = jnp.sqrt(-jnp.expm1(-2.0 * decay_rate))
    product = keys_feat * values_feat
    forward = local_pass(product, decay_rate, gain_in, residue)
    grad_float = grad_out.astype(jnp.float32)
    grad_conv = grad_float * queries
    backward = local_pass(grad_conv[::-1], decay_rate, jnp.ones_like(decay_rate), residue * gain_in)

    state_in, adjoint_in = carried_in((forward[2], backward[2]), decay_rate, length)
    conv_out = finish(forward, decay_rate, state_in) + skip_gain[None] * product
    grad_query = grad_float * conv_out
    grad_product = finish(backward, decay_rate, adjoint_in)[::-1] + skip_gain[None] * grad_conv
    grad_key = grad_product * values_feat
    grad_value = grad_product * keys_feat
    grad_stack = jnp.stack([grad_query, grad_key, grad_value])
    following = shifted(grad_stack[:, :rim_rows, :], "ctx", -1)
    padded = jnp.concatenate([grad_stack, following], axis=1)
    result = conv_taps[:, 0, None, :] * padded[:, 0:length, :]
    for shift_by in range(1, rim_rows + 1):
        result = (
            result + conv_taps[:, shift_by, None, :] * padded[:, shift_by : shift_by + length, :]
        )
    return result.astype(jnp.bfloat16)


def solution(mesh):
    in_specs = (
        P(None, "ctx", "ch"),
        P(("ctx", "ch"), None),
        P(None, None, "ch"),
        P(None, "ch"),
        P(None, "ch"),
        P("ch"),
    )
    out_specs = P(None, "ctx", "ch")
    return jax.shard_map(
        per_device, mesh=mesh, in_specs=in_specs, out_specs=out_specs, check_vma=False
    )
```

```python
import math

import jax
import jax.numpy as jnp
from jax import lax
from jax.sharding import PartitionSpec as P


def shifted(block, axis, distance):
    devices = range(lax.axis_size(axis))
    route = [(i - distance, i) for i in devices if i - distance in devices]
    return lax.ppermute(block, axis, route)


CTX = ("zz", "yy")


def carried_in(finals, decay_rate, length):
    group = lax.axis_size("yy")
    groups = lax.axis_size("zz")
    modes, width = decay_rate.shape
    part = modes // group
    mine = lax.axis_index("yy")
    rates = lax.dynamic_index_in_dim(decay_rate.reshape(group, part, width), mine, 0, False)

    def decay(distance):
        return jnp.exp(-rates * (length * distance))

    directions = (1, -1)
    pieces = jnp.stack([final.reshape(group, part, width) for final in finals], axis=1)
    members = lax.all_to_all(pieces, "yy", 0, 0, tiled=True)
    locals_, totals = [], []
    for which, step in enumerate(directions):
        member = [members[position, which] for position in range(group)]
        if step < 0:
            member = member[::-1]
        prefix = [jnp.zeros_like(member[0])]
        for position in range(1, group):
            prefix.append(decay(1.0) * prefix[-1] + member[position - 1])
        total = decay(1.0) * prefix[-1] + member[group - 1]
        if step < 0:
            prefix = prefix[::-1]
        locals_.append(prefix)
        totals.append(total)
    totals = list(lax.optimization_barrier(tuple(totals)))
    entering = []
    for total, step in zip(totals, directions):
        value = shifted(total, "zz", step)
        if groups > 2:
            value = value + decay(group) * shifted(total, "zz", 2 * step)
        entering.append(value)
    distance = 2
    while distance < groups:
        entering = list(lax.optimization_barrier(tuple(entering)))
        entering = [
            value + decay(group * distance) * shifted(value, "zz", distance * step)
            for value, step in zip(entering, directions)
        ]
        distance *= 2
    results = []
    for prefix, value, step in zip(locals_, entering, directions):
        outs = []
        for position in range(group):
            lag = position if step > 0 else group - 1 - position
            outs.append(prefix[position] + decay(lag) * value)
        results.append(jnp.stack(outs))
    back = lax.all_to_all(jnp.stack(results, axis=1), "yy", 0, 0, tiled=True)
    return [back[:, which].reshape(modes, width) for which in range(len(directions))]


def local_pass(signal, decay_rate, gain_in, gain_out):
    total_len, width_dev = signal.shape
    block_len = math.gcd(16, total_len)
    block_count = total_len // block_len
    offsets = jnp.arange(block_len, dtype=jnp.float32)
    rates = decay_rate[None]
    decay_in = jnp.exp(-rates * (block_len - 1.0 - offsets)[:, None, None]) * gain_in[None]
    decay_out = jnp.exp(-rates * (offsets + 1.0)[:, None, None]) * gain_out[None]
    kernel = jnp.sum(jnp.exp(-rates * offsets[:, None, None]) * (gain_in * gain_out)[None], axis=1)
    lag_index = (
        jnp.arange(block_len, dtype=jnp.int32)[:, None]
        - jnp.arange(block_len, dtype=jnp.int32)[None, :]
    )
    toeplitz = jnp.where(
        lag_index[:, :, None] >= 0,
        kernel[jnp.maximum(lag_index, 0)],
        jnp.zeros_like(kernel[:1, None]),
    )
    blocks = signal.reshape(block_count, block_len, width_dev)
    local_out = jnp.sum(blocks[:, None, :, :] * toeplitz[None], axis=2)
    block_ends = jnp.sum(blocks[:, :, None, :] * decay_in[None], axis=1)
    block_decay = jnp.exp(-decay_rate * block_len)

    def advance(state_now, entry):
        return (block_decay * state_now + entry, state_now)

    final_state, block_starts = lax.scan(advance, jnp.zeros_like(decay_rate), block_ends)
    return (local_out, block_starts, final_state, decay_out)


def finish(pieces, decay_rate, initial):
    local_out, block_starts, final_state, decay_out = pieces
    block_count, block_len, width_dev = local_out.shape
    anchors = jnp.arange(block_count, dtype=jnp.float32) * block_len
    powers = jnp.exp(-decay_rate[None] * anchors[:, None, None])
    states = block_starts + powers * initial[None]
    result = local_out + jnp.sum(decay_out[None] * states[:, None], axis=2)
    return result.reshape(block_count * block_len, width_dev)


def per_device(features, grad_rows, conv_taps, decay_rate, residue, skip_gain):
    length = features.shape[1]
    rim_rows = conv_taps.shape[1] - 1
    grad_out = lax.all_to_all(grad_rows, "ch", split_axis=1, concat_axis=0, tiled=True)
    last_rows = features[:, length - rim_rows :, :]
    before = shifted(last_rows, CTX, 1)
    extended = jnp.concatenate([before, features], axis=1)
    featurized = conv_taps[:, 0, None, :] * extended[:, rim_rows : rim_rows + length, :]
    for shift_by in range(1, rim_rows + 1):
        featurized = (
            featurized
            + conv_taps[:, shift_by, None, :]
            * extended[:, rim_rows - shift_by : rim_rows - shift_by + length, :]
        )
    queries = featurized[0]
    keys_feat = featurized[1]
    values_feat = featurized[2]
    gain_in = jnp.sqrt(-jnp.expm1(-2.0 * decay_rate))
    product = keys_feat * values_feat
    forward = local_pass(product, decay_rate, gain_in, residue)
    grad_float = grad_out.astype(jnp.float32)
    grad_conv = grad_float * queries
    backward = local_pass(grad_conv[::-1], decay_rate, jnp.ones_like(decay_rate), residue * gain_in)

    state_in, adjoint_in = carried_in((forward[2], backward[2]), decay_rate, length)
    conv_out = finish(forward, decay_rate, state_in) + skip_gain[None] * product
    grad_query = grad_float * conv_out
    grad_product = finish(backward, decay_rate, adjoint_in)[::-1] + skip_gain[None] * grad_conv
    grad_key = grad_product * values_feat
    grad_value = grad_product * keys_feat
    grad_stack = jnp.stack([grad_query, grad_key, grad_value])
    following = shifted(grad_stack[:, :rim_rows, :], CTX, -1)
    padded = jnp.concatenate([grad_stack, following], axis=1)
    result = conv_taps[:, 0, None, :] * padded[:, 0:length, :]
    for shift_by in range(1, rim_rows + 1):
        result = (
            result + conv_taps[:, shift_by, None, :] * padded[:, shift_by : shift_by + length, :]
        )
    return result.astype(jnp.bfloat16)


def solution(mesh):
    count = mesh.shape["ctx"]
    group = 4 if count % 4 == 0 and count > 4 else 1
    split = jax.sharding.Mesh(
        mesh.devices.reshape(count // group, group, mesh.shape["ch"]), ("zz", "yy", "ch")
    )
    in_specs = (
        P(None, CTX, "ch"),
        P((*CTX, "ch"), None),
        P(None, None, "ch"),
        P(None, "ch"),
        P(None, "ch"),
        P("ch"),
    )
    out_specs = P(None, CTX, "ch")
    return jax.shard_map(
        per_device, mesh=split, in_specs=in_specs, out_specs=out_specs, check_vma=False
    )
```

```python
import math

import jax
import jax.numpy as jnp
from jax import lax
from jax.sharding import PartitionSpec as P


def shifted(block, axis, distance):
    devices = range(lax.axis_size(axis))
    route = [(i - distance, i) for i in devices if i - distance in devices]
    return lax.ppermute(block, axis, route)


CTX = ("zz", "yy")


def carried_in(finals, decay_rate, length):
    group = lax.axis_size("yy")
    groups = lax.axis_size("zz")
    modes, width = decay_rate.shape
    part = modes // group
    mine = lax.axis_index("yy")
    rates = lax.dynamic_index_in_dim(decay_rate.reshape(group, part, width), mine, 0, False)

    def decay(distance):
        return jnp.exp(-rates * (length * distance))

    directions = (1, -1)
    pieces = jnp.stack([final.reshape(group, part, width) for final in finals], axis=1)
    members = lax.all_to_all(pieces, "yy", 0, 0, tiled=True)
    locals_, totals = [], []
    for which, step in enumerate(directions):
        member = [members[position, which] for position in range(group)]
        if step < 0:
            member = member[::-1]
        prefix = [jnp.zeros_like(member[0])]
        for position in range(1, group):
            prefix.append(decay(1.0) * prefix[-1] + member[position - 1])
        total = decay(1.0) * prefix[-1] + member[group - 1]
        if step < 0:
            prefix = prefix[::-1]
        locals_.append(prefix)
        totals.append(total)
    totals = list(lax.optimization_barrier(tuple(totals)))
    radix = 4
    entering = []
    for total, step in zip(totals, directions):
        value = shifted(total, "zz", step)
        for lag in range(2, min(radix, groups - 1) + 1):
            value = value + decay(group * (lag - 1)) * shifted(total, "zz", lag * step)
        entering.append(value)
    window = radix
    while window < groups:
        entering = list(lax.optimization_barrier(tuple(entering)))
        grown = []
        for value, step in zip(entering, directions):
            extra = value
            for part_index in range(1, radix):
                distance = part_index * window
                if distance >= groups:
                    break
                extra = extra + decay(group * distance) * shifted(value, "zz", distance * step)
            grown.append(extra)
        entering = grown
        window *= radix
    results = []
    for prefix, value, step in zip(locals_, entering, directions):
        outs = []
        for position in range(group):
            lag = position if step > 0 else group - 1 - position
            outs.append(prefix[position] + decay(lag) * value)
        results.append(jnp.stack(outs))
    back = lax.all_to_all(jnp.stack(results, axis=1), "yy", 0, 0, tiled=True)
    return [back[:, which].reshape(modes, width) for which in range(len(directions))]


def local_pass(signal, decay_rate, gain_in, gain_out):
    total_len, width_dev = signal.shape
    block_len = math.gcd(16, total_len)
    block_count = total_len // block_len
    offsets = jnp.arange(block_len, dtype=jnp.float32)
    rates = decay_rate[None]
    decay_in = jnp.exp(-rates * (block_len - 1.0 - offsets)[:, None, None]) * gain_in[None]
    decay_out = jnp.exp(-rates * (offsets + 1.0)[:, None, None]) * gain_out[None]
    kernel = jnp.sum(jnp.exp(-rates * offsets[:, None, None]) * (gain_in * gain_out)[None], axis=1)
    lag_index = (
        jnp.arange(block_len, dtype=jnp.int32)[:, None]
        - jnp.arange(block_len, dtype=jnp.int32)[None, :]
    )
    toeplitz = jnp.where(
        lag_index[:, :, None] >= 0,
        kernel[jnp.maximum(lag_index, 0)],
        jnp.zeros_like(kernel[:1, None]),
    )
    blocks = signal.reshape(block_count, block_len, width_dev)
    local_out = jnp.sum(blocks[:, None, :, :] * toeplitz[None], axis=2)
    block_ends = jnp.sum(blocks[:, :, None, :] * decay_in[None], axis=1)
    block_decay = jnp.exp(-decay_rate * block_len)

    def advance(state_now, entry):
        return (block_decay * state_now + entry, state_now)

    final_state, block_starts = lax.scan(advance, jnp.zeros_like(decay_rate), block_ends)
    return (local_out, block_starts, final_state, decay_out)


def finish(pieces, decay_rate, initial):
    local_out, block_starts, final_state, decay_out = pieces
    block_count, block_len, width_dev = local_out.shape
    anchors = jnp.arange(block_count, dtype=jnp.float32) * block_len
    powers = jnp.exp(-decay_rate[None] * anchors[:, None, None])
    states = block_starts + powers * initial[None]
    result = local_out + jnp.sum(decay_out[None] * states[:, None], axis=2)
    return result.reshape(block_count * block_len, width_dev)


def per_device(features, grad_rows, conv_taps, decay_rate, residue, skip_gain):
    length = features.shape[1]
    rim_rows = conv_taps.shape[1] - 1
    grad_out = lax.all_to_all(grad_rows, "ch", split_axis=1, concat_axis=0, tiled=True)
    last_rows = features[:, length - rim_rows :, :]
    before = shifted(last_rows, CTX, 1)
    extended = jnp.concatenate([before, features], axis=1)
    featurized = conv_taps[:, 0, None, :] * extended[:, rim_rows : rim_rows + length, :]
    for shift_by in range(1, rim_rows + 1):
        featurized = (
            featurized
            + conv_taps[:, shift_by, None, :]
            * extended[:, rim_rows - shift_by : rim_rows - shift_by + length, :]
        )
    queries = featurized[0]
    keys_feat = featurized[1]
    values_feat = featurized[2]
    gain_in = jnp.sqrt(-jnp.expm1(-2.0 * decay_rate))
    product = keys_feat * values_feat
    forward = local_pass(product, decay_rate, gain_in, residue)
    grad_float = grad_out.astype(jnp.float32)
    grad_conv = grad_float * queries
    backward = local_pass(grad_conv[::-1], decay_rate, jnp.ones_like(decay_rate), residue * gain_in)

    state_in, adjoint_in = carried_in((forward[2], backward[2]), decay_rate, length)
    conv_out = finish(forward, decay_rate, state_in) + skip_gain[None] * product
    grad_query = grad_float * conv_out
    grad_product = finish(backward, decay_rate, adjoint_in)[::-1] + skip_gain[None] * grad_conv
    grad_key = grad_product * values_feat
    grad_value = grad_product * keys_feat
    grad_stack = jnp.stack([grad_query, grad_key, grad_value])
    following = shifted(grad_stack[:, :rim_rows, :], CTX, -1)
    padded = jnp.concatenate([grad_stack, following], axis=1)
    result = conv_taps[:, 0, None, :] * padded[:, 0:length, :]
    for shift_by in range(1, rim_rows + 1):
        result = (
            result + conv_taps[:, shift_by, None, :] * padded[:, shift_by : shift_by + length, :]
        )
    return result.astype(jnp.bfloat16)


def solution(mesh):
    count = mesh.shape["ctx"]
    group = 4 if count % 4 == 0 and count > 4 else 1
    split = jax.sharding.Mesh(
        mesh.devices.reshape(count // group, group, mesh.shape["ch"]), ("zz", "yy", "ch")
    )
    in_specs = (
        P(None, CTX, "ch"),
        P((*CTX, "ch"), None),
        P(None, None, "ch"),
        P(None, "ch"),
        P(None, "ch"),
        P("ch"),
    )
    out_specs = P(None, CTX, "ch")
    return jax.shard_map(
        per_device, mesh=split, in_specs=in_specs, out_specs=out_specs, check_vma=False
    )
```

```python
import math

import jax
import jax.numpy as jnp
from jax import lax
from jax.sharding import PartitionSpec as P


def shifted(block, axis, distance):
    devices = range(lax.axis_size(axis))
    route = [(i - distance, i) for i in devices if i - distance in devices]
    return lax.ppermute(block, axis, route)


CTX = ("zz", "yy")


def split_route(groups, group, distance):
    half = group // 2
    pairs = []
    for zone in range(groups):
        for member in range(group):
            target = zone + (distance if member < half else -distance)
            if 0 <= target < groups:
                pairs.append((zone * group + member, target * group + member))
    return pairs


def carried_in(finals, decay_rate, length):
    group = lax.axis_size("yy")
    groups = lax.axis_size("zz")
    half = group // 2
    modes, width = decay_rate.shape
    part = modes // half
    mine = lax.axis_index("yy")
    forward = mine < half
    rates = lax.dynamic_index_in_dim(decay_rate.reshape(half, part, width), mine % half, 0, False)

    def decay(distance):
        return jnp.exp(-rates * (length * distance))

    pieces = jnp.concatenate([final.reshape(half, part, width) for final in finals], axis=0)
    members = lax.all_to_all(pieces, "yy", 0, 0, tiled=True)
    ordered = jnp.where(forward, members, members[::-1])
    prefix = [jnp.zeros_like(ordered[0])]
    for position in range(1, group):
        prefix.append(decay(1.0) * prefix[-1] + ordered[position - 1])
    total = decay(1.0) * prefix[-1] + ordered[group - 1]
    value = ppermute_ctx(total, split_route(groups, group, 1))
    if groups > 2:
        value = value + decay(group) * ppermute_ctx(total, split_route(groups, group, 2))
    distance = 2
    while distance < groups:
        value = value + decay(group * distance) * ppermute_ctx(
            value, split_route(groups, group, distance)
        )
        distance *= 2
    outs = jnp.stack([prefix[position] + decay(position) * value for position in range(group)])
    outs = jnp.where(forward, outs, outs[::-1])
    back = lax.all_to_all(outs, "yy", 0, 0, tiled=True)
    return [back[:half].reshape(modes, width), back[half:].reshape(modes, width)]


def ppermute_ctx(block, pairs):
    return lax.ppermute(block, CTX, pairs)


def local_pass(signal, decay_rate, gain_in, gain_out):
    total_len, width_dev = signal.shape
    block_len = math.gcd(16, total_len)
    block_count = total_len // block_len
    offsets = jnp.arange(block_len, dtype=jnp.float32)
    rates = decay_rate[None]
    decay_in = jnp.exp(-rates * (block_len - 1.0 - offsets)[:, None, None]) * gain_in[None]
    decay_out = jnp.exp(-rates * (offsets + 1.0)[:, None, None]) * gain_out[None]
    kernel = jnp.sum(jnp.exp(-rates * offsets[:, None, None]) * (gain_in * gain_out)[None], axis=1)
    lag_index = (
        jnp.arange(block_len, dtype=jnp.int32)[:, None]
        - jnp.arange(block_len, dtype=jnp.int32)[None, :]
    )
    toeplitz = jnp.where(
        lag_index[:, :, None] >= 0,
        kernel[jnp.maximum(lag_index, 0)],
        jnp.zeros_like(kernel[:1, None]),
    )
    blocks = signal.reshape(block_count, block_len, width_dev)
    local_out = jnp.sum(blocks[:, None, :, :] * toeplitz[None], axis=2)
    block_ends = jnp.sum(blocks[:, :, None, :] * decay_in[None], axis=1)
    block_decay = jnp.exp(-decay_rate * block_len)

    def advance(state_now, entry):
        return (block_decay * state_now + entry, state_now)

    final_state, block_starts = lax.scan(advance, jnp.zeros_like(decay_rate), block_ends)
    return (local_out, block_starts, final_state, decay_out)


def finish(pieces, decay_rate, initial):
    local_out, block_starts, final_state, decay_out = pieces
    block_count, block_len, width_dev = local_out.shape
    anchors = jnp.arange(block_count, dtype=jnp.float32) * block_len
    powers = jnp.exp(-decay_rate[None] * anchors[:, None, None])
    states = block_starts + powers * initial[None]
    result = local_out + jnp.sum(decay_out[None] * states[:, None], axis=2)
    return result.reshape(block_count * block_len, width_dev)


def per_device(features, grad_rows, conv_taps, decay_rate, residue, skip_gain):
    length = features.shape[1]
    rim_rows = conv_taps.shape[1] - 1
    grad_out = lax.all_to_all(grad_rows, "ch", split_axis=1, concat_axis=0, tiled=True)
    last_rows = features[:, length - rim_rows :, :]
    before = shifted(last_rows, CTX, 1)
    extended = jnp.concatenate([before, features], axis=1)
    featurized = conv_taps[:, 0, None, :] * extended[:, rim_rows : rim_rows + length, :]
    for shift_by in range(1, rim_rows + 1):
        featurized = (
            featurized
            + conv_taps[:, shift_by, None, :]
            * extended[:, rim_rows - shift_by : rim_rows - shift_by + length, :]
        )
    queries = featurized[0]
    keys_feat = featurized[1]
    values_feat = featurized[2]
    gain_in = jnp.sqrt(-jnp.expm1(-2.0 * decay_rate))
    product = keys_feat * values_feat
    forward = local_pass(product, decay_rate, gain_in, residue)
    grad_float = grad_out.astype(jnp.float32)
    grad_conv = grad_float * queries
    backward = local_pass(grad_conv[::-1], decay_rate, jnp.ones_like(decay_rate), residue * gain_in)

    state_in, adjoint_in = carried_in((forward[2], backward[2]), decay_rate, length)
    conv_out = finish(forward, decay_rate, state_in) + skip_gain[None] * product
    grad_query = grad_float * conv_out
    grad_product = finish(backward, decay_rate, adjoint_in)[::-1] + skip_gain[None] * grad_conv
    grad_key = grad_product * values_feat
    grad_value = grad_product * keys_feat
    grad_stack = jnp.stack([grad_query, grad_key, grad_value])
    following = shifted(grad_stack[:, :rim_rows, :], CTX, -1)
    padded = jnp.concatenate([grad_stack, following], axis=1)
    result = conv_taps[:, 0, None, :] * padded[:, 0:length, :]
    for shift_by in range(1, rim_rows + 1):
        result = (
            result + conv_taps[:, shift_by, None, :] * padded[:, shift_by : shift_by + length, :]
        )
    return result.astype(jnp.bfloat16)


def solution(mesh):
    count = mesh.shape["ctx"]
    group = 4 if count % 4 == 0 and count > 4 else 1
    split = jax.sharding.Mesh(
        mesh.devices.reshape(count // group, group, mesh.shape["ch"]), ("zz", "yy", "ch")
    )
    in_specs = (
        P(None, CTX, "ch"),
        P((*CTX, "ch"), None),
        P(None, None, "ch"),
        P(None, "ch"),
        P(None, "ch"),
        P("ch"),
    )
    out_specs = P(None, CTX, "ch")
    return jax.shard_map(
        per_device, mesh=split, in_specs=in_specs, out_specs=out_specs, check_vma=False
    )
```

```python
import math

import jax
import jax.numpy as jnp
from jax import lax
from jax.sharding import PartitionSpec as P


def shifted(block, axis, distance):
    devices = range(lax.axis_size(axis))
    route = [(i - distance, i) for i in devices if i - distance in devices]
    return lax.ppermute(block, axis, route)


CTX = ("zz", "yy")


def split_route(groups, group, distance):
    half = group // 2
    pairs = []
    for zone in range(groups):
        for member in range(group):
            target = zone + (distance if member < half else -distance)
            if 0 <= target < groups:
                pairs.append((zone * group + member, target * group + member))
    return pairs


def carried_in(finals, decay_rate, length):
    group = lax.axis_size("yy")
    groups = lax.axis_size("zz")
    half = group // 2
    modes, width = decay_rate.shape
    part = modes // half
    mine = lax.axis_index("yy")
    forward = mine < half
    rates = lax.dynamic_index_in_dim(decay_rate.reshape(half, part, width), mine % half, 0, False)

    def decay(distance):
        return jnp.exp(-rates * (length * distance))

    pieces = jnp.concatenate([final.reshape(half, part, width) for final in finals], axis=0)
    members = lax.all_to_all(pieces, "yy", 0, 0, tiled=True)
    ordered = jnp.where(forward, members, members[::-1])
    prefix = [jnp.zeros_like(ordered[0])]
    for position in range(1, group):
        prefix.append(decay(1.0) * prefix[-1] + ordered[position - 1])
    total = decay(1.0) * prefix[-1] + ordered[group - 1]
    value = ppermute_ctx(total, split_route(groups, group, 1))
    if groups > 2:
        value = value + decay(group) * ppermute_ctx(total, split_route(groups, group, 2))
    distance = 2
    while distance < groups:
        value = value + decay(group * distance) * ppermute_ctx(
            value, split_route(groups, group, distance)
        )
        distance *= 2
    outs = jnp.stack([prefix[position] + decay(position) * value for position in range(group)])
    outs = jnp.where(forward, outs, outs[::-1])
    back = lax.all_to_all(outs, "yy", 0, 0, tiled=True)
    return [back[:half].reshape(modes, width), back[half:].reshape(modes, width)]


def ppermute_ctx(block, pairs):
    return lax.ppermute(block, CTX, pairs)


def local_pass(signal, decay_rate, gain_in, gain_out):
    total_len, width_dev = signal.shape
    block_len = math.gcd(16, total_len)
    block_count = total_len // block_len
    offsets = jnp.arange(block_len, dtype=jnp.float32)
    rates = decay_rate[None]
    decay_in = jnp.exp(-rates * (block_len - 1.0 - offsets)[:, None, None]) * gain_in[None]
    decay_out = jnp.exp(-rates * (offsets + 1.0)[:, None, None]) * gain_out[None]
    kernel = jnp.sum(jnp.exp(-rates * offsets[:, None, None]) * (gain_in * gain_out)[None], axis=1)
    lag_index = (
        jnp.arange(block_len, dtype=jnp.int32)[:, None]
        - jnp.arange(block_len, dtype=jnp.int32)[None, :]
    )
    toeplitz = jnp.where(
        lag_index[:, :, None] >= 0,
        kernel[jnp.maximum(lag_index, 0)],
        jnp.zeros_like(kernel[:1, None]),
    )
    blocks = signal.reshape(block_count, block_len, width_dev)
    local_out = jnp.sum(blocks[:, None, :, :] * toeplitz[None], axis=2)
    block_ends = jnp.sum(blocks[:, :, None, :] * decay_in[None], axis=1)
    block_decay = jnp.exp(-decay_rate * block_len)

    state_now = jnp.zeros_like(decay_rate)
    starts = []
    for entry in range(block_count):
        starts.append(state_now)
        state_now = block_decay * state_now + block_ends[entry]
    final_state, block_starts = (state_now, jnp.stack(starts))
    return (local_out, block_starts, final_state, decay_out)


def finish(pieces, decay_rate, initial):
    local_out, block_starts, final_state, decay_out = pieces
    block_count, block_len, width_dev = local_out.shape
    anchors = jnp.arange(block_count, dtype=jnp.float32) * block_len
    powers = jnp.exp(-decay_rate[None] * anchors[:, None, None])
    states = block_starts + powers * initial[None]
    result = local_out + jnp.sum(decay_out[None] * states[:, None], axis=2)
    return result.reshape(block_count * block_len, width_dev)


def per_device(features, grad_rows, conv_taps, decay_rate, residue, skip_gain):
    length = features.shape[1]
    rim_rows = conv_taps.shape[1] - 1
    grad_out = lax.all_to_all(grad_rows, "ch", split_axis=1, concat_axis=0, tiled=True)
    last_rows = features[:, length - rim_rows :, :]
    before = shifted(last_rows, CTX, 1)
    extended = jnp.concatenate([before, features], axis=1)
    featurized = conv_taps[:, 0, None, :] * extended[:, rim_rows : rim_rows + length, :]
    for shift_by in range(1, rim_rows + 1):
        featurized = (
            featurized
            + conv_taps[:, shift_by, None, :]
            * extended[:, rim_rows - shift_by : rim_rows - shift_by + length, :]
        )
    queries = featurized[0]
    keys_feat = featurized[1]
    values_feat = featurized[2]
    gain_in = jnp.sqrt(-jnp.expm1(-2.0 * decay_rate))
    product = keys_feat * values_feat
    forward = local_pass(product, decay_rate, gain_in, residue)
    grad_float = grad_out.astype(jnp.float32)
    grad_conv = grad_float * queries
    backward = local_pass(grad_conv[::-1], decay_rate, jnp.ones_like(decay_rate), residue * gain_in)

    state_in, adjoint_in = carried_in((forward[2], backward[2]), decay_rate, length)
    conv_out = finish(forward, decay_rate, state_in) + skip_gain[None] * product
    grad_query = grad_float * conv_out
    grad_product = finish(backward, decay_rate, adjoint_in)[::-1] + skip_gain[None] * grad_conv
    grad_key = grad_product * values_feat
    grad_value = grad_product * keys_feat
    grad_stack = jnp.stack([grad_query, grad_key, grad_value])
    following = shifted(grad_stack[:, :rim_rows, :], CTX, -1)
    padded = jnp.concatenate([grad_stack, following], axis=1)
    result = conv_taps[:, 0, None, :] * padded[:, 0:length, :]
    for shift_by in range(1, rim_rows + 1):
        result = (
            result + conv_taps[:, shift_by, None, :] * padded[:, shift_by : shift_by + length, :]
        )
    return result.astype(jnp.bfloat16)


def solution(mesh):
    count = mesh.shape["ctx"]
    group = 4 if count % 4 == 0 and count > 4 else 1
    split = jax.sharding.Mesh(
        mesh.devices.reshape(count // group, group, mesh.shape["ch"]), ("zz", "yy", "ch")
    )
    in_specs = (
        P(None, CTX, "ch"),
        P((*CTX, "ch"), None),
        P(None, None, "ch"),
        P(None, "ch"),
        P(None, "ch"),
        P("ch"),
    )
    out_specs = P(None, CTX, "ch")
    return jax.shard_map(
        per_device, mesh=split, in_specs=in_specs, out_specs=out_specs, check_vma=False
    )
```

```python
import math

import jax
import jax.numpy as jnp
from jax import lax
from jax.sharding import PartitionSpec as P


def shifted(block, axis, distance):
    devices = range(lax.axis_size(axis))
    route = [(i - distance, i) for i in devices if i - distance in devices]
    return lax.ppermute(block, axis, route)


CTX = ("zz", "yy")


def split_route(groups, group, distance):
    half = group // 2
    pairs = []
    for zone in range(groups):
        for member in range(group):
            target = zone + (distance if member < half else -distance)
            if 0 <= target < groups:
                pairs.append((zone * group + member, target * group + member))
    return pairs


def carried_in(finals, decay_rate, length):
    group = lax.axis_size("yy")
    groups = lax.axis_size("zz")
    half = group // 2
    modes, width = decay_rate.shape
    part = modes // half
    mine = lax.axis_index("yy")
    forward = mine < half
    rates = lax.dynamic_index_in_dim(decay_rate.reshape(half, part, width), mine % half, 0, False)

    def decay(distance):
        return jnp.exp(-rates * (length * distance))

    pieces = jnp.concatenate([final.reshape(half, part, width) for final in finals], axis=0)
    members = lax.all_to_all(pieces, "yy", 0, 0, tiled=True)
    ordered = jnp.where(forward, members, members[::-1])
    prefix = [jnp.zeros_like(ordered[0])]
    for position in range(1, group):
        prefix.append(decay(1.0) * prefix[-1] + ordered[position - 1])
    total = decay(1.0) * prefix[-1] + ordered[group - 1]
    value = ppermute_ctx(total, split_route(groups, group, 1))
    if groups > 2:
        value = value + decay(group) * ppermute_ctx(total, split_route(groups, group, 2))
    distance = 2
    while distance < groups:
        value = value + decay(group * distance) * ppermute_ctx(
            value, split_route(groups, group, distance)
        )
        distance *= 2
    outs = jnp.stack([prefix[position] + decay(position) * value for position in range(group)])
    outs = jnp.where(forward, outs, outs[::-1])
    back = lax.all_to_all(outs, "yy", 0, 0, tiled=True)
    return [back[:half].reshape(modes, width), back[half:].reshape(modes, width)]


def ppermute_ctx(block, pairs):
    return lax.ppermute(block, CTX, pairs)


def local_pass(signal, decay_rate, gain_in, gain_out):
    total_len, width_dev = signal.shape
    block_len = math.gcd(16, total_len)
    block_count = total_len // block_len
    offsets = jnp.arange(block_len, dtype=jnp.float32)
    rates = decay_rate[None]
    decay_in = jnp.exp(-rates * (block_len - 1.0 - offsets)[:, None, None]) * gain_in[None]
    decay_out = jnp.exp(-rates * (offsets + 1.0)[:, None, None]) * gain_out[None]
    kernel = jnp.sum(jnp.exp(-rates * offsets[:, None, None]) * (gain_in * gain_out)[None], axis=1)
    lag_index = (
        jnp.arange(block_len, dtype=jnp.int32)[:, None]
        - jnp.arange(block_len, dtype=jnp.int32)[None, :]
    )
    toeplitz = jnp.where(
        lag_index[:, :, None] >= 0,
        kernel[jnp.maximum(lag_index, 0)],
        jnp.zeros_like(kernel[:1, None]),
    )
    blocks = signal.reshape(block_count, block_len, width_dev)
    local_out = jnp.sum(blocks[:, None, :, :] * toeplitz[None], axis=2)
    block_ends = jnp.sum(blocks[:, :, None, :] * decay_in[None], axis=1)
    block_decay = jnp.exp(-decay_rate * block_len)

    state_now = jnp.zeros_like(decay_rate)
    starts = []
    for entry in range(block_count):
        starts.append(state_now)
        state_now = block_decay * state_now + block_ends[entry]
    final_state, block_starts = (state_now, jnp.stack(starts))
    return (local_out, block_starts, final_state, decay_out)


def settled(pieces):
    local_out, block_starts, final_state, decay_out = pieces
    block_count, block_len, width_dev = local_out.shape
    result = local_out + jnp.sum(decay_out[None] * block_starts[:, None], axis=2)
    return result.reshape(block_count * block_len, width_dev)


def entering(decay_rate, weight, initial, length, reverse):
    offsets = jnp.arange(length, dtype=jnp.float32)
    lags = (length - offsets) if reverse else (offsets + 1.0)
    decays = jnp.exp(-decay_rate[None] * lags[:, None, None])
    return jnp.sum(decays * (weight * initial)[None], axis=1)


def per_device(features, grad_rows, conv_taps, decay_rate, residue, skip_gain):
    length = features.shape[1]
    rim_rows = conv_taps.shape[1] - 1
    grad_out = lax.all_to_all(grad_rows, "ch", split_axis=1, concat_axis=0, tiled=True)
    last_rows = features[:, length - rim_rows :, :]
    before = shifted(last_rows, CTX, 1)
    extended = jnp.concatenate([before, features], axis=1)
    featurized = conv_taps[:, 0, None, :] * extended[:, rim_rows : rim_rows + length, :]
    for shift_by in range(1, rim_rows + 1):
        featurized = (
            featurized
            + conv_taps[:, shift_by, None, :]
            * extended[:, rim_rows - shift_by : rim_rows - shift_by + length, :]
        )
    queries = featurized[0]
    keys_feat = featurized[1]
    values_feat = featurized[2]
    gain_in = jnp.sqrt(-jnp.expm1(-2.0 * decay_rate))
    product = keys_feat * values_feat
    forward = local_pass(product, decay_rate, gain_in, residue)
    grad_float = grad_out.astype(jnp.float32)
    grad_conv = grad_float * queries
    backward = local_pass(grad_conv[::-1], decay_rate, jnp.ones_like(decay_rate), residue * gain_in)

    base_out = settled(forward) + skip_gain[None] * product
    base_back = settled(backward)[::-1] + skip_gain[None] * grad_conv
    final_out, final_back, base_out, base_back = lax.optimization_barrier(
        (forward[2], backward[2], base_out, base_back)
    )
    state_in, adjoint_in = carried_in((final_out, final_back), decay_rate, length)
    conv_out = base_out + entering(decay_rate, residue, state_in, length, False)
    grad_query = grad_float * conv_out
    grad_product = base_back + entering(decay_rate, residue * gain_in, adjoint_in, length, True)
    grad_key = grad_product * values_feat
    grad_value = grad_product * keys_feat
    grad_stack = jnp.stack([grad_query, grad_key, grad_value])
    following = shifted(grad_stack[:, :rim_rows, :], CTX, -1)
    padded = jnp.concatenate([grad_stack, following], axis=1)
    result = conv_taps[:, 0, None, :] * padded[:, 0:length, :]
    for shift_by in range(1, rim_rows + 1):
        result = (
            result + conv_taps[:, shift_by, None, :] * padded[:, shift_by : shift_by + length, :]
        )
    return result.astype(jnp.bfloat16)


def solution(mesh):
    count = mesh.shape["ctx"]
    group = 4 if count % 4 == 0 and count > 4 else 1
    split = jax.sharding.Mesh(
        mesh.devices.reshape(count // group, group, mesh.shape["ch"]), ("zz", "yy", "ch")
    )
    in_specs = (
        P(None, CTX, "ch"),
        P((*CTX, "ch"), None),
        P(None, None, "ch"),
        P(None, "ch"),
        P(None, "ch"),
        P("ch"),
    )
    out_specs = P(None, CTX, "ch")
    return jax.shard_map(
        per_device, mesh=split, in_specs=in_specs, out_specs=out_specs, check_vma=False
    )
```

```python
import math

import jax
import jax.numpy as jnp
from jax import lax
from jax.sharding import PartitionSpec as P


def shifted(block, axis, distance):
    devices = range(lax.axis_size(axis))
    route = [(i - distance, i) for i in devices if i - distance in devices]
    return lax.ppermute(block, axis, route)


CTX = ("zz", "yy")


def split_route(groups, group, distance):
    half = group // 2
    pairs = []
    for zone in range(groups):
        for member in range(group):
            target = zone + (distance if member < half else -distance)
            if 0 <= target < groups:
                pairs.append((zone * group + member, target * group + member))
    return pairs


def carried_in(finals, decay_rate, length):
    group = lax.axis_size("yy")
    groups = lax.axis_size("zz")
    half = group // 2
    modes, width = decay_rate.shape
    part = modes // half
    mine = lax.axis_index("yy")
    forward = mine < half
    rates = lax.dynamic_index_in_dim(decay_rate.reshape(half, part, width), mine % half, 0, False)

    def decay(distance):
        return jnp.exp(-rates * (length * distance))

    pieces = jnp.concatenate([final.reshape(half, part, width) for final in finals], axis=0)
    members = lax.all_to_all(pieces, "yy", 0, 0, tiled=True)
    ordered = jnp.where(forward, members, members[::-1])
    prefix = [jnp.zeros_like(ordered[0])]
    for position in range(1, group):
        prefix.append(decay(1.0) * prefix[-1] + ordered[position - 1])
    total = decay(1.0) * prefix[-1] + ordered[group - 1]
    value = ppermute_ctx(total, split_route(groups, group, 1))
    if groups > 2:
        value = value + decay(group) * ppermute_ctx(total, split_route(groups, group, 2))
    distance = 2
    while distance < groups:
        value = value + decay(group * distance) * ppermute_ctx(
            value, split_route(groups, group, distance)
        )
        distance *= 2
    outs = jnp.stack([prefix[position] + decay(position) * value for position in range(group)])
    outs = jnp.where(forward, outs, outs[::-1])
    back = lax.all_to_all(outs, "yy", 0, 0, tiled=True)
    return [back[:half].reshape(modes, width), back[half:].reshape(modes, width)]


def ppermute_ctx(block, pairs):
    return lax.ppermute(block, CTX, pairs)


def local_pass(signal, decay_rate, gain_in, gain_out, reverse=False):
    total_len, width_dev = signal.shape
    block_len = math.gcd(16, total_len)
    block_count = total_len // block_len
    offsets = jnp.arange(block_len, dtype=jnp.float32)
    rates = decay_rate[None]
    lead_in = offsets if reverse else block_len - 1.0 - offsets
    lead_out = block_len - offsets if reverse else offsets + 1.0
    decay_in = jnp.exp(-rates * lead_in[:, None, None]) * gain_in[None]
    decay_out = jnp.exp(-rates * lead_out[:, None, None]) * gain_out[None]
    kernel = jnp.sum(jnp.exp(-rates * offsets[:, None, None]) * (gain_in * gain_out)[None], axis=1)
    lag_index = (
        jnp.arange(block_len, dtype=jnp.int32)[:, None]
        - jnp.arange(block_len, dtype=jnp.int32)[None, :]
    )
    if reverse:
        lag_index = -lag_index
    toeplitz = jnp.where(
        lag_index[:, :, None] >= 0,
        kernel[jnp.maximum(lag_index, 0)],
        jnp.zeros_like(kernel[:1, None]),
    )
    blocks = signal.reshape(block_count, block_len, width_dev)
    local_out = jnp.sum(blocks[:, None, :, :] * toeplitz[None], axis=2)
    block_ends = jnp.sum(blocks[:, :, None, :] * decay_in[None], axis=1)
    block_decay = jnp.exp(-decay_rate * block_len)

    state_now = jnp.zeros_like(decay_rate)
    starts = []
    order = range(block_count - 1, -1, -1) if reverse else range(block_count)
    for entry in order:
        starts.append(state_now)
        state_now = block_decay * state_now + block_ends[entry]
    if reverse:
        starts = starts[::-1]
    final_state, block_starts = (state_now, jnp.stack(starts))
    return (local_out, block_starts, final_state, decay_out)


def settled(pieces):
    local_out, block_starts, final_state, decay_out = pieces
    block_count, block_len, width_dev = local_out.shape
    result = local_out + jnp.sum(decay_out[None] * block_starts[:, None], axis=2)
    return result.reshape(block_count * block_len, width_dev)


def entering(decay_rate, weight, initial, length, reverse):
    offsets = jnp.arange(length, dtype=jnp.float32)
    lags = (length - offsets) if reverse else (offsets + 1.0)
    decays = jnp.exp(-decay_rate[None] * lags[:, None, None])
    return jnp.sum(decays * (weight * initial)[None], axis=1)


def per_device(features, grad_rows, conv_taps, decay_rate, residue, skip_gain):
    length = features.shape[1]
    rim_rows = conv_taps.shape[1] - 1
    grad_out = lax.all_to_all(grad_rows, "ch", split_axis=1, concat_axis=0, tiled=True)
    last_rows = features[:, length - rim_rows :, :]
    before = shifted(last_rows, CTX, 1)
    extended = jnp.concatenate([before, features], axis=1)
    featurized = conv_taps[:, 0, None, :] * extended[:, rim_rows : rim_rows + length, :]
    for shift_by in range(1, rim_rows + 1):
        featurized = (
            featurized
            + conv_taps[:, shift_by, None, :]
            * extended[:, rim_rows - shift_by : rim_rows - shift_by + length, :]
        )
    queries = featurized[0]
    keys_feat = featurized[1]
    values_feat = featurized[2]
    gain_in = jnp.sqrt(-jnp.expm1(-2.0 * decay_rate))
    product = keys_feat * values_feat
    forward = local_pass(product, decay_rate, gain_in, residue)
    grad_float = grad_out.astype(jnp.float32)
    grad_conv = grad_float * queries
    backward = local_pass(
        grad_conv, decay_rate, jnp.ones_like(decay_rate), residue * gain_in, reverse=True
    )

    base_out = settled(forward) + skip_gain[None] * product
    base_back = settled(backward) + skip_gain[None] * grad_conv
    final_out, final_back, base_out, base_back = lax.optimization_barrier(
        (forward[2], backward[2], base_out, base_back)
    )
    state_in, adjoint_in = carried_in((final_out, final_back), decay_rate, length)
    conv_out = base_out + entering(decay_rate, residue, state_in, length, False)
    grad_query = grad_float * conv_out
    grad_product = base_back + entering(decay_rate, residue * gain_in, adjoint_in, length, True)
    grad_key = grad_product * values_feat
    grad_value = grad_product * keys_feat
    grad_stack = jnp.stack([grad_query, grad_key, grad_value])
    following = shifted(grad_stack[:, :rim_rows, :], CTX, -1)
    padded = jnp.concatenate([grad_stack, following], axis=1)
    result = conv_taps[:, 0, None, :] * padded[:, 0:length, :]
    for shift_by in range(1, rim_rows + 1):
        result = (
            result + conv_taps[:, shift_by, None, :] * padded[:, shift_by : shift_by + length, :]
        )
    return result.astype(jnp.bfloat16)


def solution(mesh):
    count = mesh.shape["ctx"]
    group = 4 if count % 4 == 0 and count > 4 else 1
    split = jax.sharding.Mesh(
        mesh.devices.reshape(count // group, group, mesh.shape["ch"]), ("zz", "yy", "ch")
    )
    in_specs = (
        P(None, CTX, "ch"),
        P((*CTX, "ch"), None),
        P(None, None, "ch"),
        P(None, "ch"),
        P(None, "ch"),
        P("ch"),
    )
    out_specs = P(None, CTX, "ch")
    return jax.shard_map(
        per_device, mesh=split, in_specs=in_specs, out_specs=out_specs, check_vma=False
    )
```

```python
import math

import jax
import jax.numpy as jnp
from jax import lax
from jax.sharding import PartitionSpec as P


def shifted(block, axis, distance):
    devices = range(lax.axis_size(axis))
    route = [(i - distance, i) for i in devices if i - distance in devices]
    return lax.ppermute(block, axis, route)


CTX = ("zz", "yy")


def split_route(groups, group, distance):
    half = group // 2
    pairs = []
    for zone in range(groups):
        for member in range(group):
            target = zone + (distance if member < half else -distance)
            if 0 <= target < groups:
                pairs.append((zone * group + member, target * group + member))
    return pairs


def carried_in(finals, decay_rate, length, riders):
    group = lax.axis_size("yy")
    groups = lax.axis_size("zz")
    half = group // 2
    modes, width = decay_rate.shape
    part = modes // half
    mine = lax.axis_index("yy")
    forward = mine < half
    rates = lax.dynamic_index_in_dim(decay_rate.reshape(half, part, width), mine % half, 0, False)

    def decay(distance):
        return jnp.exp(-rates * (length * distance))

    pieces = jnp.concatenate([final.reshape(half, part, width) for final in finals], axis=0)
    members = lax.all_to_all(pieces, "yy", 0, 0, tiled=True)
    members, riders = lax.optimization_barrier((members, riders))
    ordered = jnp.where(forward, members, members[::-1])
    prefix = [jnp.zeros_like(ordered[0])]
    for position in range(1, group):
        prefix.append(decay(1.0) * prefix[-1] + ordered[position - 1])
    total = decay(1.0) * prefix[-1] + ordered[group - 1]
    value = ppermute_ctx(total, split_route(groups, group, 1))
    if groups > 2:
        value = value + decay(group) * ppermute_ctx(total, split_route(groups, group, 2))
    distance = 2
    while distance < groups:
        value = value + decay(group * distance) * ppermute_ctx(
            value, split_route(groups, group, distance)
        )
        distance *= 2
    outs = jnp.stack([prefix[position] + decay(position) * value for position in range(group)])
    outs = jnp.where(forward, outs, outs[::-1])
    back = lax.all_to_all(outs, "yy", 0, 0, tiled=True)
    return [back[:half].reshape(modes, width), back[half:].reshape(modes, width), riders]


def ppermute_ctx(block, pairs):
    return lax.ppermute(block, CTX, pairs)


def local_pass(signal, decay_rate, gain_in, gain_out, reverse=False):
    total_len, width_dev = signal.shape
    block_len = math.gcd(16, total_len)
    block_count = total_len // block_len
    offsets = jnp.arange(block_len, dtype=jnp.float32)
    rates = decay_rate[None]
    lead_in = offsets if reverse else block_len - 1.0 - offsets
    lead_out = block_len - offsets if reverse else offsets + 1.0
    decay_in = jnp.exp(-rates * lead_in[:, None, None]) * gain_in[None]
    decay_out = jnp.exp(-rates * lead_out[:, None, None]) * gain_out[None]
    kernel = jnp.sum(jnp.exp(-rates * offsets[:, None, None]) * (gain_in * gain_out)[None], axis=1)
    lag_index = (
        jnp.arange(block_len, dtype=jnp.int32)[:, None]
        - jnp.arange(block_len, dtype=jnp.int32)[None, :]
    )
    if reverse:
        lag_index = -lag_index
    toeplitz = jnp.where(
        lag_index[:, :, None] >= 0,
        kernel[jnp.maximum(lag_index, 0)],
        jnp.zeros_like(kernel[:1, None]),
    )
    blocks = signal.reshape(block_count, block_len, width_dev)
    local_out = jnp.sum(blocks[:, None, :, :] * toeplitz[None], axis=2)
    block_ends = jnp.sum(blocks[:, :, None, :] * decay_in[None], axis=1)
    block_decay = jnp.exp(-decay_rate * block_len)

    state_now = jnp.zeros_like(decay_rate)
    starts = []
    order = range(block_count - 1, -1, -1) if reverse else range(block_count)
    for entry in order:
        starts.append(state_now)
        state_now = block_decay * state_now + block_ends[entry]
    if reverse:
        starts = starts[::-1]
    final_state, block_starts = (state_now, jnp.stack(starts))
    return (local_out, block_starts, final_state, decay_out)


def settled(pieces):
    local_out, block_starts, final_state, decay_out = pieces
    block_count, block_len, width_dev = local_out.shape
    result = local_out + jnp.sum(decay_out[None] * block_starts[:, None], axis=2)
    return result.reshape(block_count * block_len, width_dev)


def entering(decay_rate, weight, initial, length, reverse):
    offsets = jnp.arange(length, dtype=jnp.float32)
    lags = (length - offsets) if reverse else (offsets + 1.0)
    decays = jnp.exp(-decay_rate[None] * lags[:, None, None])
    return jnp.sum(decays * (weight * initial)[None], axis=1)


def per_device(features, grad_rows, conv_taps, decay_rate, residue, skip_gain):
    length = features.shape[1]
    rim_rows = conv_taps.shape[1] - 1
    grad_out = lax.all_to_all(grad_rows, "ch", split_axis=1, concat_axis=0, tiled=True)
    last_rows = features[:, length - rim_rows :, :]
    before = shifted(last_rows, CTX, 1)
    extended = jnp.concatenate([before, features], axis=1)
    featurized = conv_taps[:, 0, None, :] * extended[:, rim_rows : rim_rows + length, :]
    for shift_by in range(1, rim_rows + 1):
        featurized = (
            featurized
            + conv_taps[:, shift_by, None, :]
            * extended[:, rim_rows - shift_by : rim_rows - shift_by + length, :]
        )
    queries = featurized[0]
    keys_feat = featurized[1]
    values_feat = featurized[2]
    gain_in = jnp.sqrt(-jnp.expm1(-2.0 * decay_rate))
    product = keys_feat * values_feat
    forward = local_pass(product, decay_rate, gain_in, residue)
    grad_float = grad_out.astype(jnp.float32)
    grad_conv = grad_float * queries
    backward = local_pass(
        grad_conv, decay_rate, jnp.ones_like(decay_rate), residue * gain_in, reverse=True
    )

    base_out = settled(forward) + skip_gain[None] * product
    base_back = settled(backward) + skip_gain[None] * grad_conv
    state_in, adjoint_in, (base_out, base_back) = carried_in(
        (forward[2], backward[2]), decay_rate, length, (base_out, base_back)
    )
    conv_out = base_out + entering(decay_rate, residue, state_in, length, False)
    grad_query = grad_float * conv_out
    grad_product = base_back + entering(decay_rate, residue * gain_in, adjoint_in, length, True)
    grad_key = grad_product * values_feat
    grad_value = grad_product * keys_feat
    grad_stack = jnp.stack([grad_query, grad_key, grad_value])
    following = shifted(grad_stack[:, :rim_rows, :], CTX, -1)
    padded = jnp.concatenate([grad_stack, following], axis=1)
    result = conv_taps[:, 0, None, :] * padded[:, 0:length, :]
    for shift_by in range(1, rim_rows + 1):
        result = (
            result + conv_taps[:, shift_by, None, :] * padded[:, shift_by : shift_by + length, :]
        )
    return result.astype(jnp.bfloat16)


def solution(mesh):
    count = mesh.shape["ctx"]
    group = 4 if count % 4 == 0 and count > 4 else 1
    split = jax.sharding.Mesh(
        mesh.devices.reshape(count // group, group, mesh.shape["ch"]), ("zz", "yy", "ch")
    )
    in_specs = (
        P(None, CTX, "ch"),
        P((*CTX, "ch"), None),
        P(None, None, "ch"),
        P(None, "ch"),
        P(None, "ch"),
        P("ch"),
    )
    out_specs = P(None, CTX, "ch")
    return jax.shard_map(
        per_device, mesh=split, in_specs=in_specs, out_specs=out_specs, check_vma=False
    )
```

```python
import math

import jax
import jax.numpy as jnp
from jax import lax
from jax.sharding import PartitionSpec as P


def shifted(block, axis, distance):
    devices = range(lax.axis_size(axis))
    route = [(i - distance, i) for i in devices if i - distance in devices]
    return lax.ppermute(block, axis, route)


CTX = ("zz", "yy")


def split_route(groups, group, distance):
    half = group // 2
    pairs = []
    for zone in range(groups):
        for member in range(group):
            target = zone + (distance if member < half else -distance)
            if 0 <= target < groups:
                pairs.append((zone * group + member, target * group + member))
    return pairs


def carried_in(finals, decay_rate, length):
    group = lax.axis_size("yy")
    groups = lax.axis_size("zz")
    half = group // 2
    modes, width = decay_rate.shape
    part = modes // half
    mine = lax.axis_index("yy")
    forward = mine < half
    rates = lax.dynamic_index_in_dim(decay_rate.reshape(half, part, width), mine % half, 0, False)

    def decay(distance):
        return jnp.exp(-rates * (length * distance))

    pieces = jnp.concatenate([final.reshape(half, part, width) for final in finals], axis=0)
    members = lax.all_to_all(pieces, "yy", 0, 0, tiled=True)
    ordered = jnp.where(forward, members, members[::-1])
    prefix = [jnp.zeros_like(ordered[0])]
    for position in range(1, group):
        prefix.append(decay(1.0) * prefix[-1] + ordered[position - 1])
    total = decay(1.0) * prefix[-1] + ordered[group - 1]
    first = min(4, groups - 1)
    value = ppermute_ctx(total, split_route(groups, group, 1))
    for lag in range(2, first + 1):
        value = value + decay(group * (lag - 1)) * ppermute_ctx(
            total, split_route(groups, group, lag)
        )
    distance = first
    while distance < groups:
        value = value + decay(group * distance) * ppermute_ctx(
            value, split_route(groups, group, distance)
        )
        distance *= 2
    outs = jnp.stack([prefix[position] + decay(position) * value for position in range(group)])
    outs = jnp.where(forward, outs, outs[::-1])
    back = lax.all_to_all(outs, "yy", 0, 0, tiled=True)
    return [back[:half].reshape(modes, width), back[half:].reshape(modes, width)]


def ppermute_ctx(block, pairs):
    return lax.ppermute(block, CTX, pairs)


def local_pass(signal, decay_rate, gain_in, gain_out, reverse=False):
    total_len, width_dev = signal.shape
    block_len = math.gcd(16, total_len)
    block_count = total_len // block_len
    offsets = jnp.arange(block_len, dtype=jnp.float32)
    rates = decay_rate[None]
    lead_in = offsets if reverse else block_len - 1.0 - offsets
    lead_out = block_len - offsets if reverse else offsets + 1.0
    decay_in = jnp.exp(-rates * lead_in[:, None, None]) * gain_in[None]
    decay_out = jnp.exp(-rates * lead_out[:, None, None]) * gain_out[None]
    kernel = jnp.sum(jnp.exp(-rates * offsets[:, None, None]) * (gain_in * gain_out)[None], axis=1)
    lag_index = (
        jnp.arange(block_len, dtype=jnp.int32)[:, None]
        - jnp.arange(block_len, dtype=jnp.int32)[None, :]
    )
    if reverse:
        lag_index = -lag_index
    toeplitz = jnp.where(
        lag_index[:, :, None] >= 0,
        kernel[jnp.maximum(lag_index, 0)],
        jnp.zeros_like(kernel[:1, None]),
    )
    blocks = signal.reshape(block_count, block_len, width_dev)
    local_out = jnp.sum(blocks[:, None, :, :] * toeplitz[None], axis=2)
    block_ends = jnp.sum(blocks[:, :, None, :] * decay_in[None], axis=1)
    block_decay = jnp.exp(-decay_rate * block_len)

    state_now = jnp.zeros_like(decay_rate)
    starts = []
    order = range(block_count - 1, -1, -1) if reverse else range(block_count)
    for entry in order:
        starts.append(state_now)
        state_now = block_decay * state_now + block_ends[entry]
    if reverse:
        starts = starts[::-1]
    final_state, block_starts = (state_now, jnp.stack(starts))
    return (local_out, block_starts, final_state, decay_out)


def settled(pieces):
    local_out, block_starts, final_state, decay_out = pieces
    block_count, block_len, width_dev = local_out.shape
    result = local_out + jnp.sum(decay_out[None] * block_starts[:, None], axis=2)
    return result.reshape(block_count * block_len, width_dev)


def entering(decay_rate, weight, initial, length, reverse):
    offsets = jnp.arange(length, dtype=jnp.float32)
    lags = (length - offsets) if reverse else (offsets + 1.0)
    decays = jnp.exp(-decay_rate[None] * lags[:, None, None])
    return jnp.sum(decays * (weight * initial)[None], axis=1)


def per_device(features, grad_rows, conv_taps, decay_rate, residue, skip_gain):
    length = features.shape[1]
    rim_rows = conv_taps.shape[1] - 1
    grad_out = lax.all_to_all(grad_rows, "ch", split_axis=1, concat_axis=0, tiled=True)
    last_rows = features[:, length - rim_rows :, :]
    before = shifted(last_rows, CTX, 1)
    extended = jnp.concatenate([before, features], axis=1)
    featurized = conv_taps[:, 0, None, :] * extended[:, rim_rows : rim_rows + length, :]
    for shift_by in range(1, rim_rows + 1):
        featurized = (
            featurized
            + conv_taps[:, shift_by, None, :]
            * extended[:, rim_rows - shift_by : rim_rows - shift_by + length, :]
        )
    queries = featurized[0]
    keys_feat = featurized[1]
    values_feat = featurized[2]
    gain_in = jnp.sqrt(-jnp.expm1(-2.0 * decay_rate))
    product = keys_feat * values_feat
    forward = local_pass(product, decay_rate, gain_in, residue)
    grad_float = grad_out.astype(jnp.float32)
    grad_conv = grad_float * queries
    backward = local_pass(
        grad_conv, decay_rate, jnp.ones_like(decay_rate), residue * gain_in, reverse=True
    )

    base_out = settled(forward) + skip_gain[None] * product
    base_back = settled(backward) + skip_gain[None] * grad_conv
    final_out, final_back, base_out, base_back = lax.optimization_barrier(
        (forward[2], backward[2], base_out, base_back)
    )
    state_in, adjoint_in = carried_in((final_out, final_back), decay_rate, length)
    conv_out = base_out + entering(decay_rate, residue, state_in, length, False)
    grad_query = grad_float * conv_out
    grad_product = base_back + entering(decay_rate, residue * gain_in, adjoint_in, length, True)
    grad_key = grad_product * values_feat
    grad_value = grad_product * keys_feat
    grad_stack = jnp.stack([grad_query, grad_key, grad_value])
    following = shifted(grad_stack[:, :rim_rows, :], CTX, -1)
    padded = jnp.concatenate([grad_stack, following], axis=1)
    result = conv_taps[:, 0, None, :] * padded[:, 0:length, :]
    for shift_by in range(1, rim_rows + 1):
        result = (
            result + conv_taps[:, shift_by, None, :] * padded[:, shift_by : shift_by + length, :]
        )
    return result.astype(jnp.bfloat16)


def solution(mesh):
    count = mesh.shape["ctx"]
    group = 4 if count % 4 == 0 and count > 4 else 1
    split = jax.sharding.Mesh(
        mesh.devices.reshape(count // group, group, mesh.shape["ch"]), ("zz", "yy", "ch")
    )
    in_specs = (
        P(None, CTX, "ch"),
        P((*CTX, "ch"), None),
        P(None, None, "ch"),
        P(None, "ch"),
        P(None, "ch"),
        P("ch"),
    )
    out_specs = P(None, CTX, "ch")
    return jax.shard_map(
        per_device, mesh=split, in_specs=in_specs, out_specs=out_specs, check_vma=False
    )
```

```python
import math

import jax
import jax.numpy as jnp
from jax import lax
from jax.sharding import PartitionSpec as P


def shifted(block, axis, distance):
    devices = range(lax.axis_size(axis))
    route = [(i - distance, i) for i in devices if i - distance in devices]
    return lax.ppermute(block, axis, route)


CTX = ("zz", "yy")


def split_route(groups, group, distance):
    half = group // 2
    pairs = []
    for zone in range(groups):
        for member in range(group):
            target = zone + (distance if member < half else -distance)
            if 0 <= target < groups:
                pairs.append((zone * group + member, target * group + member))
    return pairs


def carried_in(finals, decay_rate, length):
    group = lax.axis_size("yy")
    groups = lax.axis_size("zz")
    half = group // 2
    modes, width = decay_rate.shape
    part = modes // half
    mine = lax.axis_index("yy")
    forward = mine < half
    rates = lax.dynamic_index_in_dim(decay_rate.reshape(half, part, width), mine % half, 0, False)

    def decay(distance):
        return jnp.exp(-rates * (length * distance))

    pieces = jnp.concatenate([final.reshape(half, part, width) for final in finals], axis=0)
    members = lax.all_to_all(pieces, "yy", 0, 0, tiled=True)
    ordered = jnp.where(forward, members, members[::-1])
    prefix = [jnp.zeros_like(ordered[0])]
    for position in range(1, group):
        prefix.append(decay(1.0) * prefix[-1] + ordered[position - 1])
    total = decay(1.0) * prefix[-1] + ordered[group - 1]
    value = ppermute_ctx(total, split_route(groups, group, 1))
    if groups > 2:
        value = value + decay(group) * ppermute_ctx(total, split_route(groups, group, 2))
    distance = 2
    while distance < groups:
        value = value + decay(group * distance) * ppermute_ctx(
            value, split_route(groups, group, distance)
        )
        distance *= 2
    outs = jnp.stack([prefix[position] + decay(position) * value for position in range(group)])
    outs = jnp.where(forward, outs, outs[::-1])
    back = lax.all_to_all(outs, "yy", 0, 0, tiled=True)
    return [back[:half].reshape(modes, width), back[half:].reshape(modes, width)]


def ppermute_ctx(block, pairs):
    return lax.ppermute(block, CTX, pairs)


def local_pass(signal, decay_rate, gain_in, gain_out, reverse=False):
    total_len, width_dev = signal.shape
    block_len = math.gcd(16, total_len)
    block_count = total_len // block_len
    offsets = jnp.arange(block_len, dtype=jnp.float32)
    rates = decay_rate[None]
    lead_in = offsets if reverse else block_len - 1.0 - offsets
    lead_out = block_len - offsets if reverse else offsets + 1.0
    decay_in = jnp.exp(-rates * lead_in[:, None, None]) * gain_in[None]
    decay_out = jnp.exp(-rates * lead_out[:, None, None]) * gain_out[None]
    kernel = jnp.sum(jnp.exp(-rates * offsets[:, None, None]) * (gain_in * gain_out)[None], axis=1)
    lag_index = (
        jnp.arange(block_len, dtype=jnp.int32)[:, None]
        - jnp.arange(block_len, dtype=jnp.int32)[None, :]
    )
    if reverse:
        lag_index = -lag_index
    toeplitz = jnp.where(
        lag_index[:, :, None] >= 0,
        kernel[jnp.maximum(lag_index, 0)],
        jnp.zeros_like(kernel[:1, None]),
    )
    blocks = signal.reshape(block_count, block_len, width_dev)
    local_out = jnp.sum(blocks[:, None, :, :] * toeplitz[None], axis=2)
    block_ends = jnp.sum(blocks[:, :, None, :] * decay_in[None], axis=1)
    block_decay = jnp.exp(-decay_rate * block_len)

    state_now = jnp.zeros_like(decay_rate)
    starts = []
    order = range(block_count - 1, -1, -1) if reverse else range(block_count)
    for entry in order:
        starts.append(state_now)
        state_now = block_decay * state_now + block_ends[entry]
    if reverse:
        starts = starts[::-1]
    final_state, block_starts = (state_now, jnp.stack(starts))
    return (local_out, block_starts, final_state, decay_out)


def settled(pieces):
    local_out, block_starts, final_state, decay_out = pieces
    block_count, block_len, width_dev = local_out.shape
    result = local_out + jnp.sum(decay_out[None] * block_starts[:, None], axis=2)
    return result.reshape(block_count * block_len, width_dev)


def entering(pieces, decay_rate, initial, reverse):
    local_out, block_starts, final_state, decay_out = pieces
    block_count, block_len, width_dev = local_out.shape
    anchors = jnp.arange(block_count, dtype=jnp.float32) * block_len
    if reverse:
        anchors = anchors[::-1]
    powers = jnp.exp(-decay_rate[None] * anchors[:, None, None])
    states = powers * initial[None]
    result = jnp.sum(decay_out[None] * states[:, None], axis=2)
    return result.reshape(block_count * block_len, width_dev)


def per_device(features, grad_rows, conv_taps, decay_rate, residue, skip_gain):
    length = features.shape[1]
    rim_rows = conv_taps.shape[1] - 1
    grad_out = lax.all_to_all(grad_rows, "ch", split_axis=1, concat_axis=0, tiled=True)
    last_rows = features[:, length - rim_rows :, :]
    before = shifted(last_rows, CTX, 1)
    extended = jnp.concatenate([before, features], axis=1)
    featurized = conv_taps[:, 0, None, :] * extended[:, rim_rows : rim_rows + length, :]
    for shift_by in range(1, rim_rows + 1):
        featurized = (
            featurized
            + conv_taps[:, shift_by, None, :]
            * extended[:, rim_rows - shift_by : rim_rows - shift_by + length, :]
        )
    queries = featurized[0]
    keys_feat = featurized[1]
    values_feat = featurized[2]
    gain_in = jnp.sqrt(-jnp.expm1(-2.0 * decay_rate))
    product = keys_feat * values_feat
    forward = local_pass(product, decay_rate, gain_in, residue)
    grad_float = grad_out.astype(jnp.float32)
    grad_conv = grad_float * queries
    backward = local_pass(
        grad_conv, decay_rate, jnp.ones_like(decay_rate), residue * gain_in, reverse=True
    )

    base_out = settled(forward) + skip_gain[None] * product
    base_back = settled(backward) + skip_gain[None] * grad_conv
    final_out, final_back, base_out, base_back = lax.optimization_barrier(
        (forward[2], backward[2], base_out, base_back)
    )
    state_in, adjoint_in = carried_in((final_out, final_back), decay_rate, length)
    conv_out = base_out + entering(forward, decay_rate, state_in, False)
    grad_query = grad_float * conv_out
    grad_product = base_back + entering(backward, decay_rate, adjoint_in, True)
    grad_key = grad_product * values_feat
    grad_value = grad_product * keys_feat
    grad_stack = jnp.stack([grad_query, grad_key, grad_value])
    following = shifted(grad_stack[:, :rim_rows, :], CTX, -1)
    padded = jnp.concatenate([grad_stack, following], axis=1)
    result = conv_taps[:, 0, None, :] * padded[:, 0:length, :]
    for shift_by in range(1, rim_rows + 1):
        result = (
            result + conv_taps[:, shift_by, None, :] * padded[:, shift_by : shift_by + length, :]
        )
    return result.astype(jnp.bfloat16)


def solution(mesh):
    count = mesh.shape["ctx"]
    group = 4 if count % 4 == 0 and count > 4 else 1
    split = jax.sharding.Mesh(
        mesh.devices.reshape(count // group, group, mesh.shape["ch"]), ("zz", "yy", "ch")
    )
    in_specs = (
        P(None, CTX, "ch"),
        P((*CTX, "ch"), None),
        P(None, None, "ch"),
        P(None, "ch"),
        P(None, "ch"),
        P("ch"),
    )
    out_specs = P(None, CTX, "ch")
    return jax.shard_map(
        per_device, mesh=split, in_specs=in_specs, out_specs=out_specs, check_vma=False
    )
```

```python
import math

import jax
import jax.numpy as jnp
from jax import lax
from jax.sharding import PartitionSpec as P


def shifted(block, axis, distance):
    devices = range(lax.axis_size(axis))
    route = [(i - distance, i) for i in devices if i - distance in devices]
    return lax.ppermute(block, axis, route)


CTX = ("zz", "yy")


def split_route(groups, group, distance):
    half = group // 2
    pairs = []
    for zone in range(groups):
        for member in range(group):
            target = zone + (distance if member < half else -distance)
            if 0 <= target < groups:
                pairs.append((zone * group + member, target * group + member))
    return pairs


def carried_in(finals, decay_rate, length):
    group = lax.axis_size("yy")
    groups = lax.axis_size("zz")
    half = group // 2
    modes, width = decay_rate.shape
    part = modes // half
    mine = lax.axis_index("yy")
    forward = mine < half
    rates = lax.dynamic_index_in_dim(decay_rate.reshape(half, part, width), mine % half, 0, False)

    def decay(distance):
        return jnp.exp(-rates * (length * distance))

    pieces = jnp.concatenate([final.reshape(half, part, width) for final in finals], axis=0)
    members = lax.all_to_all(pieces, "yy", 0, 0, tiled=True)
    ordered = jnp.where(forward, members, members[::-1])
    prefix = [jnp.zeros_like(ordered[0])]
    for position in range(1, group):
        prefix.append(decay(1.0) * prefix[-1] + ordered[position - 1])
    total = decay(1.0) * prefix[-1] + ordered[group - 1]
    value = ppermute_ctx(total, split_route(groups, group, 1))
    if groups > 2:
        value = value + decay(group) * ppermute_ctx(total, split_route(groups, group, 2))
    distance = 2
    while distance < groups:
        value = value + decay(group * distance) * ppermute_ctx(
            value, split_route(groups, group, distance)
        )
        distance *= 2
    outs = jnp.stack([prefix[position] + decay(position) * value for position in range(group)])
    outs = jnp.where(forward, outs, outs[::-1])
    back = lax.all_to_all(outs, "yy", 0, 0, tiled=True)
    return [back[:half].reshape(modes, width), back[half:].reshape(modes, width)]


def ppermute_ctx(block, pairs):
    return lax.ppermute(block, CTX, pairs)


def local_pass(signal, decay_rate, gain_in, gain_out, reverse=False):
    total_len, width_dev = signal.shape
    block_len = math.gcd(16, total_len)
    block_count = total_len // block_len
    offsets = jnp.arange(block_len, dtype=jnp.float32)
    rates = decay_rate[None]
    lead_in = offsets if reverse else block_len - 1.0 - offsets
    lead_out = block_len - offsets if reverse else offsets + 1.0
    decay_in = jnp.exp(-rates * lead_in[:, None, None]) * gain_in[None]
    decay_out = jnp.exp(-rates * lead_out[:, None, None]) * gain_out[None]
    kernel = jnp.sum(jnp.exp(-rates * offsets[:, None, None]) * (gain_in * gain_out)[None], axis=1)
    lag_index = (
        jnp.arange(block_len, dtype=jnp.int32)[:, None]
        - jnp.arange(block_len, dtype=jnp.int32)[None, :]
    )
    if reverse:
        lag_index = -lag_index
    toeplitz = jnp.where(
        lag_index[:, :, None] >= 0,
        kernel[jnp.maximum(lag_index, 0)],
        jnp.zeros_like(kernel[:1, None]),
    )
    blocks = signal.reshape(block_count, block_len, width_dev)
    local_out = jnp.sum(blocks[:, None, :, :] * toeplitz[None], axis=2)
    block_ends = jnp.sum(blocks[:, :, None, :] * decay_in[None], axis=1)
    block_decay = jnp.exp(-decay_rate * block_len)

    state_now = jnp.zeros_like(decay_rate)
    starts = []
    order = range(block_count - 1, -1, -1) if reverse else range(block_count)
    for entry in order:
        starts.append(state_now)
        state_now = block_decay * state_now + block_ends[entry]
    if reverse:
        starts = starts[::-1]
    final_state, block_starts = (state_now, jnp.stack(starts))
    return (local_out, block_starts, final_state, decay_out)


def settled(pieces):
    local_out, block_starts, final_state, decay_out = pieces
    block_count, block_len, width_dev = local_out.shape
    result = local_out + jnp.sum(decay_out[None] * block_starts[:, None], axis=2)
    return result.reshape(block_count * block_len, width_dev)


def entering(decay_rate, weight, initial, length, reverse, rows=None):
    offsets = jnp.arange(length if rows is None else rows, dtype=jnp.float32)
    lags = (length - offsets) if reverse else (offsets + 1.0)
    decays = jnp.exp(-decay_rate[None] * lags[:, None, None])
    return jnp.sum(decays * (weight * initial)[None], axis=1)


def per_device(features, grad_rows, conv_taps, decay_rate, residue, skip_gain):
    length = features.shape[1]
    rim_rows = conv_taps.shape[1] - 1
    grad_out = lax.all_to_all(grad_rows, "ch", split_axis=1, concat_axis=0, tiled=True)
    last_rows = features[:, length - rim_rows :, :]
    before = shifted(last_rows, CTX, 1)
    extended = jnp.concatenate([before, features], axis=1)
    featurized = conv_taps[:, 0, None, :] * extended[:, rim_rows : rim_rows + length, :]
    for shift_by in range(1, rim_rows + 1):
        featurized = (
            featurized
            + conv_taps[:, shift_by, None, :]
            * extended[:, rim_rows - shift_by : rim_rows - shift_by + length, :]
        )
    queries = featurized[0]
    keys_feat = featurized[1]
    values_feat = featurized[2]
    gain_in = jnp.sqrt(-jnp.expm1(-2.0 * decay_rate))
    product = keys_feat * values_feat
    forward = local_pass(product, decay_rate, gain_in, residue)
    grad_float = grad_out.astype(jnp.float32)
    grad_conv = grad_float * queries
    backward = local_pass(
        grad_conv, decay_rate, jnp.ones_like(decay_rate), residue * gain_in, reverse=True
    )

    base_out = settled(forward) + skip_gain[None] * product
    base_back = settled(backward) + skip_gain[None] * grad_conv
    final_out, final_back, base_out, base_back = lax.optimization_barrier(
        (forward[2], backward[2], base_out, base_back)
    )
    state_in, adjoint_in = carried_in((final_out, final_back), decay_rate, length)
    head_query = grad_float[:rim_rows] * (
        base_out[:rim_rows] + entering(decay_rate, residue, state_in, length, False, rim_rows)
    )
    head_product = base_back[:rim_rows] + entering(
        decay_rate, residue * gain_in, adjoint_in, length, True, rim_rows
    )
    head = jnp.stack(
        [head_query, head_product * values_feat[:rim_rows], head_product * keys_feat[:rim_rows]]
    )
    following = shifted(head, CTX, -1)
    state_in, adjoint_in = lax.optimization_barrier((state_in, adjoint_in, head))[:2]
    conv_out = base_out + entering(decay_rate, residue, state_in, length, False)
    grad_query = grad_float * conv_out
    grad_product = base_back + entering(decay_rate, residue * gain_in, adjoint_in, length, True)
    grad_key = grad_product * values_feat
    grad_value = grad_product * keys_feat
    grad_stack = jnp.stack([grad_query, grad_key, grad_value])
    padded = jnp.concatenate([grad_stack, following], axis=1)
    result = conv_taps[:, 0, None, :] * padded[:, 0:length, :]
    for shift_by in range(1, rim_rows + 1):
        result = (
            result + conv_taps[:, shift_by, None, :] * padded[:, shift_by : shift_by + length, :]
        )
    return result.astype(jnp.bfloat16)


def solution(mesh):
    count = mesh.shape["ctx"]
    group = 4 if count % 4 == 0 and count > 4 else 1
    split = jax.sharding.Mesh(
        mesh.devices.reshape(count // group, group, mesh.shape["ch"]), ("zz", "yy", "ch")
    )
    in_specs = (
        P(None, CTX, "ch"),
        P((*CTX, "ch"), None),
        P(None, None, "ch"),
        P(None, "ch"),
        P(None, "ch"),
        P("ch"),
    )
    out_specs = P(None, CTX, "ch")
    return jax.shard_map(
        per_device, mesh=split, in_specs=in_specs, out_specs=out_specs, check_vma=False
    )
```

```python
import math

import jax
import jax.numpy as jnp
from jax import lax
from jax.sharding import PartitionSpec as P


def shifted(block, axis, distance):
    devices = range(lax.axis_size(axis))
    route = [(i - distance, i) for i in devices if i - distance in devices]
    return lax.ppermute(block, axis, route)


CTX = ("zz", "yy")


def split_route(groups, group, distance):
    half = group // 2
    pairs = []
    for zone in range(groups):
        for member in range(group):
            target = zone + (distance if member < half else -distance)
            if 0 <= target < groups:
                pairs.append((zone * group + member, target * group + member))
    return pairs


def carried_in(finals, decay_rate, length, riders):
    group = lax.axis_size("yy")
    groups = lax.axis_size("zz")
    half = group // 2
    modes, width = decay_rate.shape
    part = modes // half
    mine = lax.axis_index("yy")
    forward = mine < half
    rates = lax.dynamic_index_in_dim(decay_rate.reshape(half, part, width), mine % half, 0, False)

    def decay(distance):
        return jnp.exp(-rates * (length * distance))

    pieces = jnp.concatenate([final.reshape(half, part, width) for final in finals], axis=0)
    members = lax.all_to_all(pieces, "yy", 0, 0, tiled=True)
    ordered = jnp.where(forward, members, members[::-1])
    prefix = [jnp.zeros_like(ordered[0])]
    for position in range(1, group):
        prefix.append(decay(1.0) * prefix[-1] + ordered[position - 1])
    total = decay(1.0) * prefix[-1] + ordered[group - 1]
    value = ppermute_ctx(total, split_route(groups, group, 1))
    if groups > 2:
        value = value + decay(group) * ppermute_ctx(total, split_route(groups, group, 2))
    distance = 2
    while distance < groups:
        value = value + decay(group * distance) * ppermute_ctx(
            value, split_route(groups, group, distance)
        )
        distance *= 2
    outs = jnp.stack([prefix[position] + decay(position) * value for position in range(group)])
    outs = jnp.where(forward, outs, outs[::-1])
    back = lax.all_to_all(outs, "yy", 0, 0, tiled=True)
    back, riders = lax.optimization_barrier((back, riders))
    return [back[:half].reshape(modes, width), back[half:].reshape(modes, width), riders]


def ppermute_ctx(block, pairs):
    return lax.ppermute(block, CTX, pairs)


def local_pass(signal, decay_rate, gain_in, gain_out, reverse=False):
    total_len, width_dev = signal.shape
    block_len = math.gcd(16, total_len)
    block_count = total_len // block_len
    offsets = jnp.arange(block_len, dtype=jnp.float32)
    rates = decay_rate[None]
    lead_in = offsets if reverse else block_len - 1.0 - offsets
    lead_out = block_len - offsets if reverse else offsets + 1.0
    decay_in = jnp.exp(-rates * lead_in[:, None, None]) * gain_in[None]
    decay_out = jnp.exp(-rates * lead_out[:, None, None]) * gain_out[None]
    kernel = jnp.sum(jnp.exp(-rates * offsets[:, None, None]) * (gain_in * gain_out)[None], axis=1)
    lag_index = (
        jnp.arange(block_len, dtype=jnp.int32)[:, None]
        - jnp.arange(block_len, dtype=jnp.int32)[None, :]
    )
    if reverse:
        lag_index = -lag_index
    toeplitz = jnp.where(
        lag_index[:, :, None] >= 0,
        kernel[jnp.maximum(lag_index, 0)],
        jnp.zeros_like(kernel[:1, None]),
    )
    blocks = signal.reshape(block_count, block_len, width_dev)
    local_out = jnp.sum(blocks[:, None, :, :] * toeplitz[None], axis=2)
    block_ends = jnp.sum(blocks[:, :, None, :] * decay_in[None], axis=1)
    block_decay = jnp.exp(-decay_rate * block_len)

    state_now = jnp.zeros_like(decay_rate)
    starts = []
    order = range(block_count - 1, -1, -1) if reverse else range(block_count)
    for entry in order:
        starts.append(state_now)
        state_now = block_decay * state_now + block_ends[entry]
    if reverse:
        starts = starts[::-1]
    final_state, block_starts = (state_now, jnp.stack(starts))
    return (local_out, block_starts, final_state, decay_out)


def settled(pieces):
    local_out, block_starts, final_state, decay_out = pieces
    block_count, block_len, width_dev = local_out.shape
    result = local_out + jnp.sum(decay_out[None] * block_starts[:, None], axis=2)
    return result.reshape(block_count * block_len, width_dev)


def entering(decay_rate, weight, initial, length, reverse, rows=None):
    offsets = jnp.arange(length if rows is None else rows, dtype=jnp.float32)
    lags = (length - offsets) if reverse else (offsets + 1.0)
    decays = jnp.exp(-decay_rate[None] * lags[:, None, None])
    return jnp.sum(decays * (weight * initial)[None], axis=1)


def per_device(features, grad_rows, conv_taps, decay_rate, residue, skip_gain):
    length = features.shape[1]
    rim_rows = conv_taps.shape[1] - 1
    grad_out = lax.all_to_all(grad_rows, "ch", split_axis=1, concat_axis=0, tiled=True)
    last_rows = features[:, length - rim_rows :, :]
    before = shifted(last_rows, CTX, 1)
    extended = jnp.concatenate([before, features], axis=1)
    featurized = conv_taps[:, 0, None, :] * extended[:, rim_rows : rim_rows + length, :]
    for shift_by in range(1, rim_rows + 1):
        featurized = (
            featurized
            + conv_taps[:, shift_by, None, :]
            * extended[:, rim_rows - shift_by : rim_rows - shift_by + length, :]
        )
    queries = featurized[0]
    keys_feat = featurized[1]
    values_feat = featurized[2]
    gain_in = jnp.sqrt(-jnp.expm1(-2.0 * decay_rate))
    product = keys_feat * values_feat
    forward = local_pass(product, decay_rate, gain_in, residue)
    grad_float = grad_out.astype(jnp.float32)
    grad_conv = grad_float * queries
    backward = local_pass(
        grad_conv, decay_rate, jnp.ones_like(decay_rate), residue * gain_in, reverse=True
    )

    base_out = settled(forward) + skip_gain[None] * product
    base_back = settled(backward) + skip_gain[None] * grad_conv
    state_in, adjoint_in, (base_out, base_back) = carried_in(
        (forward[2], backward[2]), decay_rate, length, (base_out, base_back)
    )
    head_query = grad_float[:rim_rows] * (
        base_out[:rim_rows] + entering(decay_rate, residue, state_in, length, False, rim_rows)
    )
    head_product = base_back[:rim_rows] + entering(
        decay_rate, residue * gain_in, adjoint_in, length, True, rim_rows
    )
    head = jnp.stack(
        [head_query, head_product * values_feat[:rim_rows], head_product * keys_feat[:rim_rows]]
    )
    following = shifted(head, CTX, -1)
    state_in, adjoint_in = lax.optimization_barrier((state_in, adjoint_in, head))[:2]
    conv_out = base_out + entering(decay_rate, residue, state_in, length, False)
    grad_query = grad_float * conv_out
    grad_product = base_back + entering(decay_rate, residue * gain_in, adjoint_in, length, True)
    grad_key = grad_product * values_feat
    grad_value = grad_product * keys_feat
    grad_stack = jnp.stack([grad_query, grad_key, grad_value])
    padded = jnp.concatenate([grad_stack, following], axis=1)
    result = conv_taps[:, 0, None, :] * padded[:, 0:length, :]
    for shift_by in range(1, rim_rows + 1):
        result = (
            result + conv_taps[:, shift_by, None, :] * padded[:, shift_by : shift_by + length, :]
        )
    return result.astype(jnp.bfloat16)


def solution(mesh):
    count = mesh.shape["ctx"]
    group = 4 if count % 4 == 0 and count > 4 else 1
    split = jax.sharding.Mesh(
        mesh.devices.reshape(count // group, group, mesh.shape["ch"]), ("zz", "yy", "ch")
    )
    in_specs = (
        P(None, CTX, "ch"),
        P((*CTX, "ch"), None),
        P(None, None, "ch"),
        P(None, "ch"),
        P(None, "ch"),
        P("ch"),
    )
    out_specs = P(None, CTX, "ch")
    return jax.shard_map(
        per_device, mesh=split, in_specs=in_specs, out_specs=out_specs, check_vma=False
    )
```
